32 devices in a mesh: groups: 2 (over y), segment: 4 (over z), dp: 4 (over x, core).
Axes of the slice: x: 2, y: 2, z: 4, core: 2. Of those that a mesh axis runs over, the one named last changes fastest.
Arguments:
- fields: bfloat16 [256, 1024], P(('groups', 'dp')), parts along dimension 0, may hold values from -6 to 6
- targets: bfloat16 [256, 1024], P(('groups', 'dp')), parts along dimension 0, may hold values from -6 to 6
- neighbours: int32 [256, 4], P(('groups', 'dp')), parts along dimension 0, may hold values from 0 to 7
- weights: bfloat16 [2, 4, 1024, 1024], P(None, 'segment'), may hold values from -0.1875 to 0.1875
- gains: float32 [2, 4, 1024], P(None, 'segment'), may hold values from 0.5 to 2
Outputs:
- grad_weights: bfloat16 [4, 4, 1024, 1024], P('groups', 'segment', 'dp'), parts along dimension 0
The draws below stay inside these ranges and needn't reach their ends.
There are 2 independent parts, one for each index of `groups`. The reference program is written for one: setup_inputs(seed, part) draws one part's arguments, and reference() takes and returns one part's arrays. A program takes and returns all parts, laid end to end along the dimension named above; an argument that names none is the same for every part. Nothing has to cross between parts.
Inputs may be any that keep to these rules, and one draw needn't show every extreme that they name: `neighbours`: positions, counted within the token's own microbatch of 8 rows, of its 4 neighbouring patches.
All inputs are finite; a program needn't handle non-finite values.
Results may differ from the reference program's by a relative error of at most 0.025.
Values may be sent and summed in bfloat16 or wider, within the bound.
No kernel may reach another device: no remote copies, remote signals or barrier semaphores. Data moves between devices by JAX's collectives and lax.ppermute only.
A program may use at most 64 MiB of HBM per device.

```python
import math
import jax
import jax.numpy as jnp
from jax import lax

D = 1024
ROWS = 8
NBR = 4
MB = 4
TOKENS = 128
N_SEGMENT = 4
N_DP = 4


def plant(entries, own_key, least, high):
    longest = entries.shape.index(max(entries.shape))
    spots = []
    for shift in (0, 1):
        where = [jax.random.randint(jax.random.fold_in(own_key, axis), (), 0, length) for axis, length in enumerate(entries.shape)]
        where[longest] = (where[longest] + shift) % entries.shape[longest]
        spots.append(tuple(where))
    return entries.at[spots[0]].set(least).at[spots[1]].set(high)


def strengthened(values, own_key, source, target, shards_of, factor):
    owner, partner = [(jnp.arange(values.shape[axis_at]) // (values.shape[axis_at] // shards_of)).reshape([-1 if axis == axis_at else 1 for axis in range(values.ndim)]) for axis_at in (source, target)]
    chosen = jax.random.permutation(own_key, shards_of)[partner]
    strong = (owner == chosen) | (owner == (partner + shards_of // 2) % shards_of)
    return jnp.where(strong, factor * values, values)


def block_levels(own_key, dims, shards, smallest, top_value):
    gain = 1.0
    for axis_at, parts in shards:
        draws = jax.random.uniform(jax.random.fold_in(jax.random.fold_in(own_key, 6), axis_at), (parts,), jnp.float32, smallest / len(shards), top_value / len(shards))
        gain = gain * jnp.repeat(jnp.exp(draws), dims[axis_at] // parts).reshape((-1,) + (1,) * (len(dims) - 1 - axis_at))
    return gain


def scatter_about(own_key, extent, width, most, shards=(), kind=jnp.bfloat16):
    values = width * jax.random.normal(own_key, extent, jnp.float32)
    if shards:
        values = values * block_levels(own_key, extent, shards, -0.22, 0.18)
    return jnp.clip(values, -most, most).astype(kind)


def heavy_noise(stream_key, extent, width, reach, cuts, heavy, held_as=jnp.bfloat16):
    array = width * jax.random.normal(stream_key, extent, jnp.float32)
    if cuts:
        array = array * block_levels(stream_key, extent, cuts, -0.22, 0.18)
    return jnp.clip(strengthened(array, jax.random.fold_in(stream_key, 3), *heavy), -reach, reach).astype(held_as)


def setup_inputs(seed: int = 0, part: int = 0) -> dict:
    keys = jax.random.split(jax.random.key(seed), 6)
    part_splits = jax.random.split(jax.random.fold_in(keys[5], part), 6)
    return {
        "fields": heavy_noise(part_splits[0], (TOKENS, D), 1.0, 6.0, ((0, 4),), (0, 1, 4, 2.0)),
        "targets": scatter_about(part_splits[1], (TOKENS, D), 1.0, 6.0, ((0, 4),)),
        "neighbours": plant(jax.random.randint(part_splits[2], (TOKENS, NBR), 0, ROWS), jax.random.fold_in(part_splits[2], 1), 0, ROWS - 1).astype(jnp.int32),
        "weights": scatter_about(keys[3], (2, N_SEGMENT, D, D), D ** -0.5, 0.1875, ((1, 4),)),
        "gains": jnp.clip(jnp.exp(math.log(2.0) - 1.3862944 * jax.random.uniform(keys[4], (2, N_SEGMENT, D), jnp.float32) ** block_levels(keys[4], (2, N_SEGMENT, D), ((1, 4),), -0.2, 0.2)), 0.5, 2.0),
    }


EPSILON = 1e-06

def mixing_matrix(neighbour_rows):
    positions = jnp.arange(neighbour_rows.shape[0], dtype=jnp.int32)
    matches = (neighbour_rows[:, :, None] == positions[None, None, :]).astype(jnp.float32)
    return lax.optimization_barrier(jnp.sum(matches, axis=1)) * (0.5 / neighbour_rows.shape[1])

def layer_forward(residual, weight, gain_row, mixing):
    widened = residual.astype(jnp.float32)
    inverse = lax.rsqrt(lax.optimization_barrier(jnp.mean(widened * widened, axis=-1, keepdims=True)) + EPSILON)
    normed = widened * inverse * gain_row
    blended = 0.5 * normed + jnp.dot(mixing, normed, precision=lax.Precision.HIGHEST)
    active = blended.astype(jnp.bfloat16)
    before = jnp.dot(active, weight, preferred_element_type=jnp.float32)
    return ((widened + jnp.tanh(before)).astype(jnp.bfloat16), active, before)

def layer_backward(residual, before, weight, gain_row, mixing, upper_grad):
    widened = residual.astype(jnp.float32)
    inverse = lax.rsqrt(lax.optimization_barrier(jnp.mean(widened * widened, axis=-1, keepdims=True)) + EPSILON)
    above = upper_grad.astype(jnp.float32)
    squashed = jnp.tanh(before)
    dbefore = (above * (1.0 - squashed * squashed)).astype(jnp.bfloat16)
    dblend = jnp.dot(dbefore, weight.T, preferred_element_type=jnp.float32)
    dnormed = (0.5 * dblend + jnp.dot(mixing.T, dblend, precision=lax.Precision.HIGHEST)) * gain_row
    inner_mean = lax.optimization_barrier(jnp.mean(dnormed * widened, axis=-1, keepdims=True))
    lower_grad = above + inverse * dnormed - widened * (inverse * inverse * inverse) * inner_mean
    return (lower_grad.astype(jnp.bfloat16), dbefore)

def reference(fields, targets, neighbours, weights, gains):
    layer_count = 2 * N_SEGMENT
    scale_top = 1.0 / math.sqrt(TOKENS)
    field_groups = fields.reshape(N_DP, MB, ROWS, D)
    target_groups = targets.reshape(N_DP, MB, ROWS, D)
    neighbour_groups = neighbours.reshape(N_DP, MB, ROWS, NBR)

    def one_micro(inputs):
        source, target, neighbour_rows = inputs
        mixing = mixing_matrix(neighbour_rows)
        saved = []
        residual = source
        for layer in range(layer_count):
            phase, place = divmod(layer, N_SEGMENT)
            result, active, before = layer_forward(residual, weights[phase, place], gains[phase, place], mixing)
            saved.append((residual, active, before))
            residual = result
        upper_grad = ((residual.astype(jnp.float32) - target.astype(jnp.float32)) * scale_top).astype(jnp.bfloat16)
        actives = [None] * layer_count
        dpres = [None] * layer_count
        for layer in reversed(range(layer_count)):
            phase, place = divmod(layer, N_SEGMENT)
            upper_grad, dbefore = layer_backward(saved[layer][0], saved[layer][2], weights[phase, place], gains[phase, place], mixing, upper_grad)
            actives[layer] = saved[layer][1]
            dpres[layer] = dbefore
        return (jnp.stack(actives), jnp.stack(dpres))

    def one_group(total, inputs):
        actives, dpres = lax.map(one_micro, inputs)
        partial_sum = jnp.einsum('mlrd,mlre->lde', actives.astype(jnp.float32), dpres.astype(jnp.float32))
        rounded = lax.optimization_barrier(partial_sum.astype(jnp.bfloat16)).astype(jnp.float32)
        return (total + rounded.reshape(2, N_SEGMENT, D, D), None)
    start = jnp.zeros((2, N_SEGMENT, D, D), jnp.float32)
    total, _ = lax.scan(one_group, start, (field_groups, target_groups, neighbour_groups))
    return total.astype(jnp.bfloat16)
```

```python
import math

import jax
import jax.numpy as jnp
from jax import lax
from jax.sharding import PartitionSpec as P

ROWS = 8


EPSILON = 1e-06


def mixing_blocks(neighbour_rows):
    positions = jnp.arange(neighbour_rows.shape[1], dtype=jnp.int32)
    matches = (neighbour_rows[:, :, :, None] == positions[None, None, None, :]).astype(jnp.float32)
    return jnp.sum(matches, axis=2) * (0.5 / neighbour_rows.shape[2])


def mix_apply(mixing, values):
    micro = mixing.shape[0]
    blocks = values.reshape(micro, ROWS, values.shape[-1])
    mixed = jnp.einsum("bik,bkd->bid", mixing, blocks, precision=lax.Precision.HIGHEST)
    return mixed.reshape(values.shape)


def mix_apply_t(mixing, values):
    micro = mixing.shape[0]
    blocks = values.reshape(micro, ROWS, values.shape[-1])
    mixed = jnp.einsum("bki,bkd->bid", mixing, blocks, precision=lax.Precision.HIGHEST)
    return mixed.reshape(values.shape)


def layer_forward(residual, weight, gain_row, mixing):
    widened = residual.astype(jnp.float32)
    inverse = lax.rsqrt(jnp.mean(widened * widened, axis=-1, keepdims=True) + EPSILON)
    normed = widened * inverse * gain_row
    blended = 0.5 * normed + mix_apply(mixing, normed)
    active = blended.astype(jnp.bfloat16)
    before = jnp.dot(active, weight, preferred_element_type=jnp.float32)
    squashed = jnp.tanh(before)
    return ((widened + squashed).astype(jnp.bfloat16), active, squashed, inverse)


def layer_backward(residual, squashed, inverse, weight, gain_row, mixing, upper_grad):
    widened = residual.astype(jnp.float32)
    above = upper_grad.astype(jnp.float32)
    dbefore = (above * (1.0 - squashed * squashed)).astype(jnp.bfloat16)
    dblend = lax.dot_general(
        dbefore, weight, (((1,), (1,)), ((), ())), preferred_element_type=jnp.float32
    )
    dnormed = (0.5 * dblend + mix_apply_t(mixing, dblend)) * gain_row
    inner_mean = jnp.mean(dnormed * widened, axis=-1, keepdims=True)
    lower_grad = above + inverse * dnormed - widened * (inverse * inverse * inverse) * inner_mean
    return (lower_grad.astype(jnp.bfloat16), dbefore)


def hop(array, source, target):
    return lax.ppermute(array, "segment", [(source, target)])


def on_device(fields, targets, neighbours, weights, gains):
    segments = lax.axis_size("segment")
    data_groups = lax.axis_size("dp")
    place = lax.axis_index("segment")
    group = lax.axis_index("dp")
    tokens, width = fields.shape
    micro_count = tokens // ROWS
    scale_top = 1.0 / math.sqrt(tokens * data_groups)
    mixing = mixing_blocks(neighbours.reshape(micro_count, ROWS, neighbours.shape[1]))
    weight_pair = weights[:, 0]
    gain_pair = gains[:, 0]
    layer_count = 2 * segments

    state = fields
    saved = [None, None]
    for layer in range(layer_count):
        phase, member = divmod(layer, segments)
        result, active, squashed, inverse = layer_forward(
            state, weight_pair[phase], gain_pair[phase], mixing
        )
        values = (state, active, squashed, inverse)
        if member == 0:
            saved[phase] = values
        else:
            mine = place == member
            saved[phase] = tuple(jnp.where(mine, new, old) for new, old in zip(values, saved[phase]))
        if layer + 1 < layer_count:
            state = hop(result, layer % segments, (layer + 1) % segments)
        else:
            state = result

    upper = ((state.astype(jnp.float32) - targets.astype(jnp.float32)) * scale_top).astype(jnp.bfloat16)

    dpre_saved = [None, None]
    for layer in reversed(range(layer_count)):
        phase, member = divmod(layer, segments)
        residual, _, squashed, inverse = saved[phase]
        lower, dbefore = layer_backward(
            residual, squashed, inverse, weight_pair[phase], gain_pair[phase], mixing, upper
        )
        if member == segments - 1:
            dpre_saved[phase] = dbefore
        else:
            dpre_saved[phase] = jnp.where(place == member, dbefore, dpre_saved[phase])
        if layer > 0:
            upper = hop(lower, layer % segments, (layer - 1) % segments)

    rows = width // data_groups
    grads = []
    for phase in range(2):
        dpre_mine = dpre_saved[phase]
        act_mine = saved[phase][1]
        dpre_all = lax.all_gather(dpre_mine, "dp", tiled=True)
        act_all = lax.all_gather(act_mine, "dp", tiled=True)
        act_rows = lax.dynamic_slice_in_dim(act_all, group * rows, rows, axis=1)
        grads.append(
            lax.dot_general(
                act_rows, dpre_all, (((0,), (0,)), ((), ())), preferred_element_type=jnp.float32
            ).astype(jnp.bfloat16)
        )
    return jnp.stack(grads)[:, None]


def solution(mesh):
    return jax.shard_map(
        on_device,
        mesh=mesh,
        in_specs=(
            P(("groups", "dp"), None),
            P(("groups", "dp"), None),
            P(("groups", "dp"), None),
            P(None, "segment", None, None),
            P(None, "segment", None),
        ),
        out_specs=P("groups", "segment", "dp", None),
        check_vma=False,
    )
```

```python
import math

import jax
import jax.numpy as jnp
from jax import lax
from jax.experimental import pallas as pl
from jax.experimental.pallas import tpu as pltpu
from jax.sharding import PartitionSpec as P

ROWS = 8
EPSILON = 1e-06
BLOCK = 256


def split3(values):
    high = values.astype(jnp.bfloat16)
    rest = values - high.astype(jnp.float32)
    middle = rest.astype(jnp.bfloat16)
    low = (rest - middle.astype(jnp.float32)).astype(jnp.bfloat16)
    return high, middle, low


def exact_mix(matrix, values):
    total = None
    for piece in split3(values):
        part = jnp.dot(matrix, piece, preferred_element_type=jnp.float32)
        total = part if total is None else total + part
    return total


def mixing_rows(nbr):
    tokens, count = nbr.shape
    row = lax.broadcasted_iota(jnp.int32, (tokens, tokens), 0)
    col = lax.broadcasted_iota(jnp.int32, (tokens, tokens), 1)
    base = jnp.bitwise_and(row, -ROWS)
    hits = jnp.zeros((tokens, tokens), jnp.float32)
    for k in range(count):
        hits = hits + jnp.where(nbr[:, k:k + 1] + base == col, 1.0, 0.0)
    return (hits * (0.5 / count)).astype(jnp.bfloat16)


def mixing_cols(nbr_t):
    count, tokens = nbr_t.shape
    row = lax.broadcasted_iota(jnp.int32, (tokens, tokens), 0)
    col = lax.broadcasted_iota(jnp.int32, (tokens, tokens), 1)
    base = jnp.bitwise_and(col, -ROWS)
    hits = jnp.zeros((tokens, tokens), jnp.float32)
    for k in range(count):
        hits = hits + jnp.where(nbr_t[k:k + 1, :] + base == row, 1.0, 0.0)
    return (hits * (0.5 / count)).astype(jnp.bfloat16)


def forward_kernel(x_ref, xb_ref, nbr_ref, gain_ref, w_ref, y_ref, act_ref, sq_ref, act_scr):
    @pl.when(pl.program_id(0) == 0)
    def _():
        widened = x_ref[...].astype(jnp.float32)
        inverse = lax.rsqrt(jnp.mean(widened * widened, axis=-1, keepdims=True) + EPSILON)
        normed = widened * inverse * gain_ref[...]
        blended = 0.5 * normed + exact_mix(mixing_rows(nbr_ref[...]), normed)
        active = blended.astype(jnp.bfloat16)
        act_scr[...] = active
        act_ref[...] = active

    before = jnp.dot(act_scr[...], w_ref[...], preferred_element_type=jnp.float32)
    squashed = jnp.tanh(before)
    sq_ref[...] = squashed
    y_ref[...] = (xb_ref[...].astype(jnp.float32) + squashed).astype(jnp.bfloat16)


def layer_forward(residual, weights, gains, phase, nbr):
    tokens, width = residual.shape
    block = min(BLOCK, width)
    steps = width // block
    full = lambda shape: pl.BlockSpec(shape, lambda j: (0, 0))
    return pl.pallas_call(
        forward_kernel,
        grid=(steps,),
        in_specs=[
            full((tokens, width)),
            pl.BlockSpec((tokens, block), lambda j: (0, j)),
            full(nbr.shape),
            pl.BlockSpec((None, 1, width), lambda j: (phase, 0, 0)),
            pl.BlockSpec((None, None, width, block), lambda j: (phase, 0, 0, j)),
        ],
        out_specs=[
            pl.BlockSpec((tokens, block), lambda j: (0, j)),
            full((tokens, width)),
            pl.BlockSpec((tokens, block), lambda j: (0, j)),
        ],
        out_shape=[
            jax.ShapeDtypeStruct((tokens, width), jnp.bfloat16),
            jax.ShapeDtypeStruct((tokens, width), jnp.bfloat16),
            jax.ShapeDtypeStruct((tokens, width), jnp.float32),
        ],
        scratch_shapes=[pltpu.VMEM((tokens, width), jnp.bfloat16)],
        compiler_params=pltpu.CompilerParams(dimension_semantics=("arbitrary",)),
        cost_estimate=pl.CostEstimate(
            flops=2 * tokens * width * width, transcendentals=tokens * width,
            bytes_accessed=2 * width * width + 12 * tokens * width,
        ),
    )(residual, residual, nbr, gains, weights)


def backward_kernel(up_ref, sq_ref, x_ref, nbr_t_ref, gain_ref, w_ref, low_ref, dpre_ref, dpre_scr, dmix_scr):
    step = pl.program_id(0)
    steps = pl.num_programs(0)

    @pl.when(step == 0)
    def _():
        above = up_ref[...].astype(jnp.float32)
        squashed = sq_ref[...]
        dbefore = (above * (1.0 - squashed * squashed)).astype(jnp.bfloat16)
        dpre_scr[...] = dbefore
        dpre_ref[...] = dbefore

    part = lax.dot_general(
        dpre_scr[...], w_ref[...], (((1,), (1,)), ((), ())), preferred_element_type=jnp.float32
    )
    dmix_scr[step] = part

    @pl.when(step == steps - 1)
    def _():
        count = dmix_scr.shape[0]
        dblend = jnp.concatenate([dmix_scr[k] for k in range(count)], axis=1)
        dnormed = (0.5 * dblend + exact_mix(mixing_cols(nbr_t_ref[...]), dblend)) * gain_ref[...]
        widened = x_ref[...].astype(jnp.float32)
        inverse = lax.rsqrt(jnp.mean(widened * widened, axis=-1, keepdims=True) + EPSILON)
        inner_mean = jnp.mean(dnormed * widened, axis=-1, keepdims=True)
        above = up_ref[...].astype(jnp.float32)
        lower = above + inverse * dnormed - widened * (inverse * inverse * inverse) * inner_mean
        low_ref[...] = lower.astype(jnp.bfloat16)


def layer_backward(residual, squashed, weights, gains, phase, nbr_t, upper_grad):
    tokens, width = residual.shape
    block = min(BLOCK, width)
    steps = width // block
    full = lambda shape: pl.BlockSpec(shape, lambda j: (0, 0))
    return pl.pallas_call(
        backward_kernel,
        grid=(steps,),
        in_specs=[
            full((tokens, width)),
            full((tokens, width)),
            full((tokens, width)),
            full(nbr_t.shape),
            pl.BlockSpec((None, 1, width), lambda j: (phase, 0, 0)),
            pl.BlockSpec((None, None, block, width), lambda j: (phase, 0, j, 0)),
        ],
        out_specs=[full((tokens, width)), full((tokens, width))],
        out_shape=[
            jax.ShapeDtypeStruct((tokens, width), jnp.bfloat16),
            jax.ShapeDtypeStruct((tokens, width), jnp.bfloat16),
        ],
        scratch_shapes=[
            pltpu.VMEM((tokens, width), jnp.bfloat16),
            pltpu.VMEM((steps, tokens, block), jnp.float32),
        ],
        compiler_params=pltpu.CompilerParams(dimension_semantics=("arbitrary",)),
        cost_estimate=pl.CostEstimate(
            flops=2 * tokens * width * width, transcendentals=0,
            bytes_accessed=2 * width * width + 14 * tokens * width,
        ),
    )(upper_grad, squashed, residual, nbr_t, gains, weights)


def hop(array, source, target):
    return lax.ppermute(array, "segment", [(source, target)])


def on_device(fields, targets, neighbours, weights, gains):
    segments = lax.axis_size("segment")
    data_groups = lax.axis_size("dp")
    place = lax.axis_index("segment")
    group = lax.axis_index("dp")
    tokens, width = fields.shape
    scale_top = 1.0 / math.sqrt(tokens * data_groups)
    neighbours_t = neighbours.T
    layer_count = 2 * segments

    state = fields
    saved = [None, None]
    for layer in range(layer_count):
        phase, member = divmod(layer, segments)
        result, active, squashed = layer_forward(state, weights, gains, phase, neighbours)
        values = (state, active, squashed)
        if member == 0:
            saved[phase] = values
        else:
            mine = place == member
            saved[phase] = tuple(jnp.where(mine, new, old) for new, old in zip(values, saved[phase]))
        if layer + 1 < layer_count:
            state = hop(result, layer % segments, (layer + 1) % segments)
        else:
            state = result

    upper = ((state.astype(jnp.float32) - targets.astype(jnp.float32)) * scale_top).astype(jnp.bfloat16)

    dpre_saved = [None, None]
    for layer in reversed(range(layer_count)):
        phase, member = divmod(layer, segments)
        residual, _, squashed = saved[phase]
        if layer > 0:
            lower, dbefore = layer_backward(
                residual, squashed, weights, gains, phase, neighbours_t, upper
            )
        else:
            dbefore = (upper.astype(jnp.float32) * (1.0 - squashed * squashed)).astype(jnp.bfloat16)
        if member == segments - 1:
            dpre_saved[phase] = dbefore
        else:
            dpre_saved[phase] = jnp.where(place == member, dbefore, dpre_saved[phase])
        if layer > 0:
            upper = hop(lower, layer % segments, (layer - 1) % segments)

    rows = width // data_groups
    grads = []
    for phase in range(2):
        dpre_all = lax.all_gather(dpre_saved[phase], "dp", tiled=True)
        act_all = lax.all_gather(saved[phase][1], "dp", tiled=True)
        act_rows = lax.dynamic_slice_in_dim(act_all, group * rows, rows, axis=1)
        grads.append(
            lax.dot_general(
                act_rows, dpre_all, (((0,), (0,)), ((), ())), preferred_element_type=jnp.float32
            ).astype(jnp.bfloat16)
        )
    return jnp.stack(grads)[:, None]


def solution(mesh):
    return jax.shard_map(
        on_device,
        mesh=mesh,
        in_specs=(
            P(("groups", "dp"), None),
            P(("groups", "dp"), None),
            P(("groups", "dp"), None),
            P(None, "segment", None, None),
            P(None, "segment", None),
        ),
        out_specs=P("groups", "segment", "dp", None),
        check_vma=False,
    )
```

```python
import math

import jax
import jax.numpy as jnp
from jax import lax
from jax.experimental import pallas as pl
from jax.experimental.pallas import tpu as pltpu
from jax.sharding import PartitionSpec as P

ROWS = 8


EPSILON = 1e-06


def mixing_blocks(neighbour_rows):
    positions = jnp.arange(neighbour_rows.shape[1], dtype=jnp.int32)
    matches = (neighbour_rows[:, :, :, None] == positions[None, None, None, :]).astype(jnp.float32)
    return jnp.sum(matches, axis=2) * (0.5 / neighbour_rows.shape[2])


def mix_apply(mixing, values):
    micro = mixing.shape[0]
    blocks = values.reshape(micro, ROWS, values.shape[-1])
    mixed = jnp.einsum("bik,bkd->bid", mixing, blocks, precision=lax.Precision.HIGHEST)
    return mixed.reshape(values.shape)


def mix_apply_t(mixing, values):
    micro = mixing.shape[0]
    blocks = values.reshape(micro, ROWS, values.shape[-1])
    mixed = jnp.einsum("bki,bkd->bid", mixing, blocks, precision=lax.Precision.HIGHEST)
    return mixed.reshape(values.shape)


def layer_forward(residual, weight, gain_row, mixing):
    widened = residual.astype(jnp.float32)
    inverse = lax.rsqrt(jnp.mean(widened * widened, axis=-1, keepdims=True) + EPSILON)
    normed = widened * inverse * gain_row
    blended = 0.5 * normed + mix_apply(mixing, normed)
    active = blended.astype(jnp.bfloat16)
    before = jnp.dot(active, weight, preferred_element_type=jnp.float32)
    squashed = jnp.tanh(before)
    return ((widened + squashed).astype(jnp.bfloat16), active, squashed, inverse)


def layer_backward(residual, squashed, inverse, weight, gain_row, mixing, upper_grad):
    widened = residual.astype(jnp.float32)
    above = upper_grad.astype(jnp.float32)
    dbefore = (above * (1.0 - squashed * squashed)).astype(jnp.bfloat16)
    dblend = lax.dot_general(
        dbefore, weight, (((1,), (1,)), ((), ())), preferred_element_type=jnp.float32
    )
    dnormed = (0.5 * dblend + mix_apply_t(mixing, dblend)) * gain_row
    inner_mean = jnp.mean(dnormed * widened, axis=-1, keepdims=True)
    lower_grad = above + inverse * dnormed - widened * (inverse * inverse * inverse) * inner_mean
    return (lower_grad.astype(jnp.bfloat16), dbefore)


def fetch_kernel(phase, weights_hbm, out_vmem, sem):
    copy = pltpu.make_async_copy(weights_hbm.at[phase, 0], out_vmem, sem)
    copy.start()
    copy.wait()


def resident_weight(weights, phase):
    width = weights.shape[-1]
    return pl.pallas_call(
        lambda *refs: fetch_kernel(phase, *refs),
        in_specs=[pl.BlockSpec(memory_space=pl.ANY)],
        out_specs=pl.BlockSpec(memory_space=pltpu.VMEM),
        out_shape=jax.ShapeDtypeStruct((width, width), weights.dtype),
        scratch_shapes=[pltpu.SemaphoreType.DMA(())],
    )(weights)


def hop(array, source, target):
    return lax.ppermute(array, "segment", [(source, target)])


def on_device(fields, targets, neighbours, weights, gains):
    segments = lax.axis_size("segment")
    data_groups = lax.axis_size("dp")
    place = lax.axis_index("segment")
    group = lax.axis_index("dp")
    tokens, width = fields.shape
    micro_count = tokens // ROWS
    scale_top = 1.0 / math.sqrt(tokens * data_groups)
    mixing = mixing_blocks(neighbours.reshape(micro_count, ROWS, neighbours.shape[1]))
    weight_pair = [resident_weight(weights, phase) for phase in range(2)]
    gain_pair = gains[:, 0]
    layer_count = 2 * segments

    state = fields
    saved = [None, None]
    for layer in range(layer_count):
        phase, member = divmod(layer, segments)
        result, active, squashed, inverse = layer_forward(
            state, weight_pair[phase], gain_pair[phase], mixing
        )
        values = (state, active, squashed, inverse)
        if member == 0:
            saved[phase] = values
        else:
            mine = place == member
            saved[phase] = tuple(jnp.where(mine, new, old) for new, old in zip(values, saved[phase]))
        if layer + 1 < layer_count:
            state = hop(result, layer % segments, (layer + 1) % segments)
        else:
            state = result

    upper = ((state.astype(jnp.float32) - targets.astype(jnp.float32)) * scale_top).astype(jnp.bfloat16)

    dpre_saved = [None, None]
    for layer in reversed(range(layer_count)):
        phase, member = divmod(layer, segments)
        residual, _, squashed, inverse = saved[phase]
        lower, dbefore = layer_backward(
            residual, squashed, inverse, weight_pair[phase], gain_pair[phase], mixing, upper
        )
        if member == segments - 1:
            dpre_saved[phase] = dbefore
        else:
            dpre_saved[phase] = jnp.where(place == member, dbefore, dpre_saved[phase])
        if layer > 0:
            upper = hop(lower, layer % segments, (layer - 1) % segments)

    rows = width // data_groups
    grads = []
    for phase in range(2):
        dpre_mine = dpre_saved[phase]
        act_mine = saved[phase][1]
        dpre_all = lax.all_gather(dpre_mine, "dp", tiled=True)
        act_all = lax.all_gather(act_mine, "dp", tiled=True)
        act_rows = lax.dynamic_slice_in_dim(act_all, group * rows, rows, axis=1)
        grads.append(
            lax.dot_general(
                act_rows, dpre_all, (((0,), (0,)), ((), ())), preferred_element_type=jnp.float32
            ).astype(jnp.bfloat16)
        )
    return jnp.stack(grads)[:, None]


def solution(mesh):
    return jax.shard_map(
        on_device,
        mesh=mesh,
        in_specs=(
            P(("groups", "dp"), None),
            P(("groups", "dp"), None),
            P(("groups", "dp"), None),
            P(None, "segment", None, None),
            P(None, "segment", None),
        ),
        out_specs=P("groups", "segment", "dp", None),
        check_vma=False,
    )
```

```python
import math

import jax
import jax.numpy as jnp
from jax import lax
from jax.experimental import pallas as pl
from jax.experimental.pallas import tpu as pltpu
from jax.sharding import PartitionSpec as P

ROWS = 8


EPSILON = 1e-06


def mixing_blocks(neighbour_rows):
    positions = jnp.arange(neighbour_rows.shape[1], dtype=jnp.int32)
    matches = (neighbour_rows[:, :, :, None] == positions[None, None, None, :]).astype(jnp.float32)
    return jnp.sum(matches, axis=2) * (0.5 / neighbour_rows.shape[2])


def mix_apply(mixing, values):
    micro = mixing.shape[0]
    blocks = values.reshape(micro, ROWS, values.shape[-1])
    mixed = jnp.einsum("bik,bkd->bid", mixing, blocks, precision=lax.Precision.HIGHEST)
    return mixed.reshape(values.shape)


def mix_apply_t(mixing, values):
    micro = mixing.shape[0]
    blocks = values.reshape(micro, ROWS, values.shape[-1])
    mixed = jnp.einsum("bki,bkd->bid", mixing, blocks, precision=lax.Precision.HIGHEST)
    return mixed.reshape(values.shape)


def layer_forward(residual, weight, gain_row, mixing):
    widened = residual.astype(jnp.float32)
    inverse = lax.rsqrt(jnp.mean(widened * widened, axis=-1, keepdims=True) + EPSILON)
    normed = widened * inverse * gain_row
    blended = 0.5 * normed + mix_apply(mixing, normed)
    active = blended.astype(jnp.bfloat16)
    before = jnp.dot(active, weight, preferred_element_type=jnp.float32)
    squashed = jnp.tanh(before)
    return ((widened + squashed).astype(jnp.bfloat16), active, squashed, inverse)


def layer_backward(residual, squashed, inverse, weight, gain_row, mixing, upper_grad):
    widened = residual.astype(jnp.float32)
    above = upper_grad.astype(jnp.float32)
    dbefore = (above * (1.0 - squashed * squashed)).astype(jnp.bfloat16)
    dblend = lax.dot_general(
        dbefore, weight, (((1,), (1,)), ((), ())), preferred_element_type=jnp.float32
    )
    dnormed = (0.5 * dblend + mix_apply_t(mixing, dblend)) * gain_row
    inner_mean = jnp.mean(dnormed * widened, axis=-1, keepdims=True)
    lower_grad = above + inverse * dnormed - widened * (inverse * inverse * inverse) * inner_mean
    return (lower_grad.astype(jnp.bfloat16), dbefore)


def fetch_kernel(phase, weights_hbm, after_hbm, out_vmem, sem):
    del after_hbm
    copy = pltpu.make_async_copy(weights_hbm.at[phase, 0], out_vmem, sem)
    copy.start()
    copy.wait()


def resident_weight(weights, phase, after):
    width = weights.shape[-1]
    return pl.pallas_call(
        lambda *refs: fetch_kernel(phase, *refs),
        in_specs=[pl.BlockSpec(memory_space=pl.ANY), pl.BlockSpec(memory_space=pl.ANY)],
        out_specs=pl.BlockSpec(memory_space=pltpu.VMEM),
        out_shape=jax.ShapeDtypeStruct((width, width), weights.dtype),
        scratch_shapes=[pltpu.SemaphoreType.DMA(())],
    )(weights, after)


def hop(array, source, target):
    return lax.ppermute(array, "segment", [(source, target)])


def on_device(fields, targets, neighbours, weights, gains):
    segments = lax.axis_size("segment")
    data_groups = lax.axis_size("dp")
    place = lax.axis_index("segment")
    group = lax.axis_index("dp")
    tokens, width = fields.shape
    micro_count = tokens // ROWS
    scale_top = 1.0 / math.sqrt(tokens * data_groups)
    mixing = mixing_blocks(neighbours.reshape(micro_count, ROWS, neighbours.shape[1]))
    gain_pair = gains[:, 0]
    layer_count = 2 * segments

    state = fields
    saved = [None, None]
    weight_pair = [weights[0, 0], None]
    for layer in range(layer_count):
        phase, member = divmod(layer, segments)
        result, active, squashed, inverse = layer_forward(
            state, weight_pair[phase], gain_pair[phase], mixing
        )
        if layer == 0:
            weight_pair = [resident_weight(weights, 0, result), resident_weight(weights, 1, result)]
        values = (state, active, squashed, inverse)
        if member == 0:
            saved[phase] = values
        else:
            mine = place == member
            saved[phase] = tuple(jnp.where(mine, new, old) for new, old in zip(values, saved[phase]))
        if layer + 1 < layer_count:
            state = hop(result, layer % segments, (layer + 1) % segments)
        else:
            state = result

    upper = ((state.astype(jnp.float32) - targets.astype(jnp.float32)) * scale_top).astype(jnp.bfloat16)

    dpre_saved = [None, None]
    for layer in reversed(range(1, layer_count)):
        phase, member = divmod(layer, segments)
        residual, _, squashed, inverse = saved[phase]
        lower, dbefore = layer_backward(
            residual, squashed, inverse, weight_pair[phase], gain_pair[phase], mixing, upper
        )
        if member == segments - 1:
            dpre_saved[phase] = dbefore
        else:
            dpre_saved[phase] = jnp.where(place == member, dbefore, dpre_saved[phase])
        if layer > 1:
            upper = hop(lower, layer % segments, (layer - 1) % segments)

    pairs_of = lambda shift: [
        (data_groups + source, (source + shift) % data_groups) for source in range(data_groups)
    ]
    arrived = jnp.stack(
        [lax.ppermute(lower, ("segment", "dp"), pairs_of(shift)) for shift in range(data_groups)]
    )
    reversed_blocks = arrived[::-1]
    doubled = jnp.concatenate([reversed_blocks, reversed_blocks], axis=0)
    upper_all = lax.dynamic_slice_in_dim(doubled, data_groups - 1 - group, data_groups, axis=0)
    upper_all = upper_all.reshape(data_groups * tokens, width)
    squashed_all = lax.all_gather(saved[0][2], "dp", tiled=True)
    dpre_first = (
        upper_all.astype(jnp.float32) * (1.0 - squashed_all * squashed_all)
    ).astype(jnp.bfloat16)

    rows = width // data_groups
    grads = []
    for phase in range(2):
        dpre_all = lax.all_gather(dpre_saved[phase], "dp", tiled=True)
        if phase == 0:
            dpre_all = jnp.where(place == 0, dpre_first, dpre_all)
        act_all = lax.all_gather(saved[phase][1], "dp", tiled=True)
        act_rows = lax.dynamic_slice_in_dim(act_all, group * rows, rows, axis=1)
        grads.append(
            lax.dot_general(
                act_rows, dpre_all, (((0,), (0,)), ((), ())), preferred_element_type=jnp.float32
            ).astype(jnp.bfloat16)
        )
    return jnp.stack(grads)[:, None]


def solution(mesh):
    return jax.shard_map(
        on_device,
        mesh=mesh,
        in_specs=(
            P(("groups", "dp"), None),
            P(("groups", "dp"), None),
            P(("groups", "dp"), None),
            P(None, "segment", None, None),
            P(None, "segment", None),
        ),
        out_specs=P("groups", "segment", "dp", None),
        check_vma=False,
    )
```

```python
import math

import jax
import jax.numpy as jnp
from jax import lax
from jax.experimental import pallas as pl
from jax.experimental.pallas import tpu as pltpu
from jax.sharding import PartitionSpec as P

ROWS = 8


EPSILON = 1e-06


def mixing_blocks(neighbour_rows):
    positions = jnp.arange(neighbour_rows.shape[1], dtype=jnp.int32)
    matches = (neighbour_rows[:, :, :, None] == positions[None, None, None, :]).astype(jnp.float32)
    return jnp.sum(matches, axis=2) * (0.5 / neighbour_rows.shape[2])


def mix_apply(mixing, values):
    micro = mixing.shape[0]
    blocks = values.reshape(micro, ROWS, values.shape[-1])
    mixed = jnp.einsum("bik,bkd->bid", mixing, blocks, precision=lax.Precision.HIGHEST)
    return mixed.reshape(values.shape)


def mix_apply_t(mixing, values):
    micro = mixing.shape[0]
    blocks = values.reshape(micro, ROWS, values.shape[-1])
    mixed = jnp.einsum("bki,bkd->bid", mixing, blocks, precision=lax.Precision.HIGHEST)
    return mixed.reshape(values.shape)


def layer_forward(residual, weight, gain_row, mixing):
    widened = residual.astype(jnp.float32)
    inverse = lax.rsqrt(jnp.mean(widened * widened, axis=-1, keepdims=True) + EPSILON)
    normed = widened * inverse * gain_row
    blended = 0.5 * normed + mix_apply(mixing, normed)
    active = blended.astype(jnp.bfloat16)
    before = jnp.dot(active, weight, preferred_element_type=jnp.float32)
    squashed = jnp.tanh(before)
    return ((widened + squashed).astype(jnp.bfloat16), active, squashed, inverse)


def layer_backward(residual, squashed, inverse, weight, gain_row, mixing, upper_grad):
    widened = residual.astype(jnp.float32)
    above = upper_grad.astype(jnp.float32)
    dbefore = (above * (1.0 - squashed * squashed)).astype(jnp.bfloat16)
    dblend = lax.dot_general(
        dbefore, weight, (((1,), (1,)), ((), ())), preferred_element_type=jnp.float32
    )
    dnormed = (0.5 * dblend + mix_apply_t(mixing, dblend)) * gain_row
    inner_mean = jnp.mean(dnormed * widened, axis=-1, keepdims=True)
    lower_grad = above + inverse * dnormed - widened * (inverse * inverse * inverse) * inner_mean
    return (lower_grad.astype(jnp.bfloat16), dbefore)


def fetch_kernel(phase, weights_hbm, out_vmem, sem):
    copy = pltpu.make_async_copy(weights_hbm.at[phase, 0], out_vmem, sem)
    copy.start()
    copy.wait()


def resident_weight(weights, phase):
    width = weights.shape[-1]
    return pl.pallas_call(
        lambda *refs: fetch_kernel(phase, *refs),
        in_specs=[pl.BlockSpec(memory_space=pl.ANY)],
        out_specs=pl.BlockSpec(memory_space=pltpu.VMEM),
        out_shape=jax.ShapeDtypeStruct((width, width), weights.dtype),
        scratch_shapes=[pltpu.SemaphoreType.DMA(())],
    )(weights)


def hop(array, source, target):
    return lax.ppermute(array, "segment", [(source, target)])


def on_device(fields, targets, neighbours, weights, gains):
    segments = lax.axis_size("segment")
    data_groups = lax.axis_size("dp")
    place = lax.axis_index("segment")
    group = lax.axis_index("dp")
    tokens, width = fields.shape
    micro_count = tokens // ROWS
    scale_top = 1.0 / math.sqrt(tokens * data_groups)
    mixing = mixing_blocks(neighbours.reshape(micro_count, ROWS, neighbours.shape[1]))
    weight_pair = [resident_weight(weights, phase) for phase in range(2)]
    gain_pair = gains[:, 0]
    layer_count = 2 * segments

    state = fields
    saved = [None, None]
    for layer in range(layer_count):
        phase, member = divmod(layer, segments)
        result, active, squashed, inverse = layer_forward(
            state, weight_pair[phase], gain_pair[phase], mixing
        )
        values = (state, active, squashed, inverse)
        if member == 0:
            saved[phase] = values
        else:
            mine = place == member
            saved[phase] = tuple(jnp.where(mine, new, old) for new, old in zip(values, saved[phase]))
        if layer + 1 < layer_count:
            state = hop(result, layer % segments, (layer + 1) % segments)
        else:
            state = result

    upper = ((state.astype(jnp.float32) - targets.astype(jnp.float32)) * scale_top).astype(jnp.bfloat16)

    dpre_saved = [None, None]
    for layer in reversed(range(layer_count)):
        phase, member = divmod(layer, segments)
        residual, _, squashed, inverse = saved[phase]
        lower, dbefore = layer_backward(
            residual, squashed, inverse, weight_pair[phase], gain_pair[phase], mixing, upper
        )
        if member == segments - 1:
            dpre_saved[phase] = dbefore
        else:
            dpre_saved[phase] = jnp.where(place == member, dbefore, dpre_saved[phase])
        if layer > 0:
            upper = hop(lower, layer % segments, (layer - 1) % segments)

    rows = width // data_groups
    grads = []
    for phase in range(2):
        both = jnp.concatenate([saved[phase][1], dpre_saved[phase]], axis=1)
        both_all = lax.all_gather(both, "dp", tiled=True)
        act_rows = lax.dynamic_slice_in_dim(both_all, group * rows, rows, axis=1)
        dpre_all = both_all[:, width:]
        grads.append(
            lax.dot_general(
                act_rows, dpre_all, (((0,), (0,)), ((), ())), preferred_element_type=jnp.float32
            ).astype(jnp.bfloat16)
        )
    return jnp.stack(grads)[:, None]


def solution(mesh):
    return jax.shard_map(
        on_device,
        mesh=mesh,
        in_specs=(
            P(("groups", "dp"), None),
            P(("groups", "dp"), None),
            P(("groups", "dp"), None),
            P(None, "segment", None, None),
            P(None, "segment", None),
        ),
        out_specs=P("groups", "segment", "dp", None),
        check_vma=False,
    )
```

```python
import math

import jax
import jax.numpy as jnp
from jax import lax
from jax.experimental import pallas as pl
from jax.experimental.pallas import tpu as pltpu
from jax.sharding import PartitionSpec as P

ROWS = 8


EPSILON = 1e-06


def mixing_blocks(neighbour_rows):
    positions = jnp.arange(neighbour_rows.shape[1], dtype=jnp.int32)
    matches = (neighbour_rows[:, :, :, None] == positions[None, None, None, :]).astype(jnp.float32)
    return jnp.sum(matches, axis=2) * (0.5 / neighbour_rows.shape[2])


def mix_apply(mixing, values):
    micro = mixing.shape[0]
    blocks = values.reshape(micro, ROWS, values.shape[-1])
    mixed = jnp.einsum("bik,bkd->bid", mixing, blocks, precision=lax.Precision.HIGHEST)
    return mixed.reshape(values.shape)


def mix_apply_t(mixing, values):
    micro = mixing.shape[0]
    blocks = values.reshape(micro, ROWS, values.shape[-1])
    mixed = jnp.einsum("bki,bkd->bid", mixing, blocks, precision=lax.Precision.HIGHEST)
    return mixed.reshape(values.shape)


def layer_forward(residual, weight, gain_row, mixing):
    widened = residual.astype(jnp.float32)
    inverse = lax.rsqrt(jnp.mean(widened * widened, axis=-1, keepdims=True) + EPSILON)
    normed = widened * inverse * gain_row
    blended = 0.5 * normed + mix_apply(mixing, normed)
    active = blended.astype(jnp.bfloat16)
    before = jnp.dot(active, weight, preferred_element_type=jnp.float32)
    squashed = jnp.tanh(before)
    return ((widened + squashed).astype(jnp.bfloat16), active, squashed, inverse)


def layer_backward(residual, squashed, inverse, weight, gain_row, mixing, upper_grad):
    widened = residual.astype(jnp.float32)
    above = upper_grad.astype(jnp.float32)
    dbefore = (above * (1.0 - squashed * squashed)).astype(jnp.bfloat16)
    dblend = lax.dot_general(
        dbefore, weight, (((1,), (1,)), ((), ())), preferred_element_type=jnp.float32
    )
    dnormed = (0.5 * dblend + mix_apply_t(mixing, dblend)) * gain_row
    inner_mean = jnp.mean(dnormed * widened, axis=-1, keepdims=True)
    lower_grad = above + inverse * dnormed - widened * (inverse * inverse * inverse) * inner_mean
    return (lower_grad.astype(jnp.bfloat16), dbefore)


def fetch_kernel(phase, weights_hbm, out_vmem, sem):
    copy = pltpu.make_async_copy(weights_hbm.at[phase, 0], out_vmem, sem)
    copy.start()
    copy.wait()


def resident_weight(weights, phase):
    width = weights.shape[-1]
    return pl.pallas_call(
        lambda *refs: fetch_kernel(phase, *refs),
        in_specs=[pl.BlockSpec(memory_space=pl.ANY)],
        out_specs=pl.BlockSpec(memory_space=pltpu.VMEM),
        out_shape=jax.ShapeDtypeStruct((width, width), weights.dtype),
        scratch_shapes=[pltpu.SemaphoreType.DMA(())],
    )(weights)


def hop(array, source, target):
    return lax.ppermute(array, "segment", [(source, target)])


def on_device(fields, targets, neighbours, weights, gains):
    segments = lax.axis_size("segment")
    data_groups = lax.axis_size("dp")
    place = lax.axis_index("segment")
    group = lax.axis_index("dp")
    tokens, width = fields.shape
    micro_count = tokens // ROWS
    scale_top = 1.0 / math.sqrt(tokens * data_groups)
    mixing = mixing_blocks(neighbours.reshape(micro_count, ROWS, neighbours.shape[1]))
    weight_pair = [resident_weight(weights, phase) for phase in range(2)]
    gain_pair = gains[:, 0]
    layer_count = 2 * segments

    state = fields
    saved = [None, None]
    for layer in range(layer_count):
        phase, member = divmod(layer, segments)
        result, active, squashed, inverse = layer_forward(
            state, weight_pair[phase], gain_pair[phase], mixing
        )
        values = (state, active, squashed, inverse)
        if member == 0:
            saved[phase] = values
        else:
            mine = place == member
            saved[phase] = tuple(jnp.where(mine, new, old) for new, old in zip(values, saved[phase]))
        if layer + 1 < layer_count:
            state = hop(result, layer % segments, (layer + 1) % segments)
        else:
            state = result

    upper = ((state.astype(jnp.float32) - targets.astype(jnp.float32)) * scale_top).astype(jnp.bfloat16)

    dpre_saved = [None, None]
    for layer in reversed(range(layer_count)):
        phase, member = divmod(layer, segments)
        residual, _, squashed, inverse = saved[phase]
        lower, dbefore = layer_backward(
            residual, squashed, inverse, weight_pair[phase], gain_pair[phase], mixing, upper
        )
        if member == segments - 1:
            dpre_saved[phase] = dbefore
        else:
            dpre_saved[phase] = jnp.where(place == member, dbefore, dpre_saved[phase])
        if layer > 0:
            upper = hop(lower, layer % segments, (layer - 1) % segments)

    rows = width // data_groups
    early = jnp.concatenate([saved[1][1], dpre_saved[1], saved[0][1]], axis=1)
    early_all = lax.all_gather(early, "dp", tiled=True)
    late_all = lax.all_gather(dpre_saved[0], "dp", tiled=True)
    act_rows = jnp.stack([
        lax.dynamic_slice_in_dim(early_all, 2 * width + group * rows, rows, axis=1),
        lax.dynamic_slice_in_dim(early_all, group * rows, rows, axis=1),
    ])
    dpre_all = jnp.stack([late_all, early_all[:, width:2 * width]])
    grads = lax.dot_general(
        act_rows, dpre_all, (((1,), (1,)), ((0,), (0,))), preferred_element_type=jnp.float32
    ).astype(jnp.bfloat16)
    return grads[:, None]


def solution(mesh):
    return jax.shard_map(
        on_device,
        mesh=mesh,
        in_specs=(
            P(("groups", "dp"), None),
            P(("groups", "dp"), None),
            P(("groups", "dp"), None),
            P(None, "segment", None, None),
            P(None, "segment", None),
        ),
        out_specs=P("groups", "segment", "dp", None),
        check_vma=False,
    )
```

```python
import math

import jax
import jax.numpy as jnp
from jax import lax
from jax.experimental import pallas as pl
from jax.experimental.pallas import tpu as pltpu
from jax.sharding import PartitionSpec as P

ROWS = 8


EPSILON = 1e-06


def mixing_blocks(neighbour_rows):
    positions = jnp.arange(neighbour_rows.shape[1], dtype=jnp.int32)
    matches = (neighbour_rows[:, :, :, None] == positions[None, None, None, :]).astype(jnp.float32)
    return jnp.sum(matches, axis=2) * (0.5 / neighbour_rows.shape[2])


def mix_apply(mixing, values):
    micro = mixing.shape[0]
    blocks = values.reshape(micro, ROWS, values.shape[-1])
    mixed = jnp.einsum("bik,bkd->bid", mixing, blocks, precision=lax.Precision.HIGHEST)
    return mixed.reshape(values.shape)


def mix_apply_t(mixing, values):
    micro = mixing.shape[0]
    blocks = values.reshape(micro, ROWS, values.shape[-1])
    mixed = jnp.einsum("bki,bkd->bid", mixing, blocks, precision=lax.Precision.HIGHEST)
    return mixed.reshape(values.shape)


def layer_forward(residual, weight, gain_row, mixing):
    widened = residual.astype(jnp.float32)
    inverse = lax.rsqrt(jnp.mean(widened * widened, axis=-1, keepdims=True) + EPSILON)
    normed = widened * inverse * gain_row
    blended = 0.5 * normed + mix_apply(mixing, normed)
    active = blended.astype(jnp.bfloat16)
    before = jnp.dot(active, weight, preferred_element_type=jnp.float32)
    squashed = jnp.tanh(before)
    return ((widened + squashed).astype(jnp.bfloat16), active, squashed, inverse)


def layer_backward(residual, squashed, inverse, weight, gain_row, mixing, upper_grad):
    widened = residual.astype(jnp.float32)
    above = upper_grad.astype(jnp.float32)
    dbefore = (above * (1.0 - squashed * squashed)).astype(jnp.bfloat16)
    dblend = lax.dot_general(
        dbefore, weight, (((1,), (1,)), ((), ())), preferred_element_type=jnp.float32
    )
    dnormed = (0.5 * dblend + mix_apply_t(mixing, dblend)) * gain_row
    inner_mean = jnp.mean(dnormed * widened, axis=-1, keepdims=True)
    lower_grad = above + inverse * dnormed - widened * (inverse * inverse * inverse) * inner_mean
    return (lower_grad.astype(jnp.bfloat16), dbefore)


def fetch_kernel(phase, weights_hbm, out_vmem, sem):
    copy = pltpu.make_async_copy(weights_hbm.at[phase, 0], out_vmem, sem)
    copy.start()
    copy.wait()


def resident_weight(weights, phase):
    width = weights.shape[-1]
    return pl.pallas_call(
        lambda *refs: fetch_kernel(phase, *refs),
        in_specs=[pl.BlockSpec(memory_space=pl.ANY)],
        out_specs=pl.BlockSpec(memory_space=pltpu.VMEM),
        out_shape=jax.ShapeDtypeStruct((width, width), weights.dtype),
        scratch_shapes=[pltpu.SemaphoreType.DMA(())],
    )(weights)


def hop(array, source, target):
    return lax.ppermute(array, "segment", [(source, target)])


def on_device(fields, targets, neighbours, weights, gains):
    segments = lax.axis_size("segment")
    data_groups = lax.axis_size("dp")
    place = lax.axis_index("segment")
    group = lax.axis_index("dp")
    tokens, width = fields.shape
    micro_count = tokens // ROWS
    scale_top = 1.0 / math.sqrt(tokens * data_groups)
    mixing = mixing_blocks(neighbours.reshape(micro_count, ROWS, neighbours.shape[1]))
    weight_pair = [resident_weight(weights, phase) for phase in range(2)]
    gain_pair = gains[:, 0]
    layer_count = 2 * segments

    state = fields
    saved = [None, None]
    for layer in range(layer_count):
        phase, member = divmod(layer, segments)
        result, active, squashed, inverse = layer_forward(
            state, weight_pair[phase], gain_pair[phase], mixing
        )
        values = (state, active, squashed, inverse)
        if member == 0:
            saved[phase] = values
        else:
            mine = place == member
            saved[phase] = tuple(jnp.where(mine, new, old) for new, old in zip(values, saved[phase]))
        if layer + 1 < layer_count:
            state = hop(result, layer % segments, (layer + 1) % segments)
        else:
            state = result

    upper = ((state.astype(jnp.float32) - targets.astype(jnp.float32)) * scale_top).astype(jnp.bfloat16)

    dpre_saved = [None, None]
    for layer in reversed(range(layer_count)):
        phase, member = divmod(layer, segments)
        residual, _, squashed, inverse = saved[phase]
        lower, dbefore = layer_backward(
            residual, squashed, inverse, weight_pair[phase], gain_pair[phase], mixing, upper
        )
        if member == segments - 1:
            dpre_saved[phase] = dbefore
        else:
            dpre_saved[phase] = jnp.where(place == member, dbefore, dpre_saved[phase])
        if layer > 0:
            upper = hop(lower, layer % segments, (layer - 1) % segments)
        if layer == segments:
            early = jnp.concatenate([saved[1][1], dpre_saved[1], saved[0][1]], axis=1)
            early_all = lax.all_gather(early, "dp", tiled=True)
            upper, early_all = lax.optimization_barrier((upper, early_all))

    rows = width // data_groups
    late_all = lax.all_gather(dpre_saved[0], "dp", tiled=True)
    act_rows = jnp.stack([
        lax.dynamic_slice_in_dim(early_all, 2 * width + group * rows, rows, axis=1),
        lax.dynamic_slice_in_dim(early_all, group * rows, rows, axis=1),
    ])
    dpre_all = jnp.stack([late_all, early_all[:, width:2 * width]])
    grads = lax.dot_general(
        act_rows, dpre_all, (((1,), (1,)), ((0,), (0,))), preferred_element_type=jnp.float32
    ).astype(jnp.bfloat16)
    return grads[:, None]


def solution(mesh):
    return jax.shard_map(
        on_device,
        mesh=mesh,
        in_specs=(
            P(("groups", "dp"), None),
            P(("groups", "dp"), None),
            P(("groups", "dp"), None),
            P(None, "segment", None, None),
            P(None, "segment", None),
        ),
        out_specs=P("groups", "segment", "dp", None),
        check_vma=False,
    )
```

```python
import math

import jax
import jax.numpy as jnp
from jax import lax
from jax.experimental import pallas as pl
from jax.experimental.pallas import tpu as pltpu
from jax.sharding import PartitionSpec as P

ROWS = 8


EPSILON = 1e-06


def mixing_blocks(neighbour_rows):
    positions = jnp.arange(neighbour_rows.shape[1], dtype=jnp.int32)
    matches = (neighbour_rows[:, :, :, None] == positions[None, None, None, :]).astype(jnp.float32)
    return jnp.sum(matches, axis=2) * (0.5 / neighbour_rows.shape[2])


def mix_apply(mixing, values):
    micro = mixing.shape[0]
    blocks = values.reshape(micro, ROWS, values.shape[-1])
    mixed = jnp.sum(mixing[:, :, :, None] * blocks[:, None, :, :], axis=2)
    return mixed.reshape(values.shape)


def mix_apply_t(mixing, values):
    micro = mixing.shape[0]
    blocks = values.reshape(micro, ROWS, values.shape[-1])
    mixed = jnp.sum(mixing[:, :, :, None] * blocks[:, :, None, :], axis=1)
    return mixed.reshape(values.shape)


def layer_forward(residual, weight, gain_row, mixing):
    widened = residual.astype(jnp.float32)
    inverse = lax.rsqrt(jnp.mean(widened * widened, axis=-1, keepdims=True) + EPSILON)
    normed = widened * inverse * gain_row
    blended = 0.5 * normed + mix_apply(mixing, normed)
    active = blended.astype(jnp.bfloat16)
    before = jnp.dot(active, weight, preferred_element_type=jnp.float32)
    squashed = jnp.tanh(before)
    return ((widened + squashed).astype(jnp.bfloat16), active, squashed, inverse)


def layer_backward(residual, squashed, inverse, weight, gain_row, mixing, upper_grad):
    widened = residual.astype(jnp.float32)
    above = upper_grad.astype(jnp.float32)
    dbefore = (above * (1.0 - squashed * squashed)).astype(jnp.bfloat16)
    dblend = lax.dot_general(
        dbefore, weight, (((1,), (1,)), ((), ())), preferred_element_type=jnp.float32
    )
    dnormed = (0.5 * dblend + mix_apply_t(mixing, dblend)) * gain_row
    inner_mean = jnp.mean(dnormed * widened, axis=-1, keepdims=True)
    lower_grad = above + inverse * dnormed - widened * (inverse * inverse * inverse) * inner_mean
    return (lower_grad.astype(jnp.bfloat16), dbefore)


def fetch_kernel(phase, weights_hbm, out_vmem, sem):
    copy = pltpu.make_async_copy(weights_hbm.at[phase, 0], out_vmem, sem)
    copy.start()
    copy.wait()


def resident_weight(weights, phase):
    width = weights.shape[-1]
    return pl.pallas_call(
        lambda *refs: fetch_kernel(phase, *refs),
        in_specs=[pl.BlockSpec(memory_space=pl.ANY)],
        out_specs=pl.BlockSpec(memory_space=pltpu.VMEM),
        out_shape=jax.ShapeDtypeStruct((width, width), weights.dtype),
        scratch_shapes=[pltpu.SemaphoreType.DMA(())],
    )(weights)


def hop(array, source, target):
    return lax.ppermute(array, "segment", [(source, target)])


def on_device(fields, targets, neighbours, weights, gains):
    segments = lax.axis_size("segment")
    data_groups = lax.axis_size("dp")
    place = lax.axis_index("segment")
    group = lax.axis_index("dp")
    tokens, width = fields.shape
    micro_count = tokens // ROWS
    scale_top = 1.0 / math.sqrt(tokens * data_groups)
    mixing = mixing_blocks(neighbours.reshape(micro_count, ROWS, neighbours.shape[1]))
    weight_pair = [resident_weight(weights, phase) for phase in range(2)]
    gain_pair = gains[:, 0]
    layer_count = 2 * segments

    state = fields
    saved = [None, None]
    for layer in range(layer_count):
        phase, member = divmod(layer, segments)
        result, active, squashed, inverse = layer_forward(
            state, weight_pair[phase], gain_pair[phase], mixing
        )
        values = (state, active, squashed, inverse)
        if member == 0:
            saved[phase] = values
        else:
            mine = place == member
            saved[phase] = tuple(jnp.where(mine, new, old) for new, old in zip(values, saved[phase]))
        if layer + 1 < layer_count:
            state = hop(result, layer % segments, (layer + 1) % segments)
        else:
            state = result

    upper = ((state.astype(jnp.float32) - targets.astype(jnp.float32)) * scale_top).astype(jnp.bfloat16)

    dpre_saved = [None, None]
    for layer in reversed(range(layer_count)):
        phase, member = divmod(layer, segments)
        residual, _, squashed, inverse = saved[phase]
        lower, dbefore = layer_backward(
            residual, squashed, inverse, weight_pair[phase], gain_pair[phase], mixing, upper
        )
        if member == segments - 1:
            dpre_saved[phase] = dbefore
        else:
            dpre_saved[phase] = jnp.where(place == member, dbefore, dpre_saved[phase])
        if layer > 0:
            upper = hop(lower, layer % segments, (layer - 1) % segments)
        if layer == segments:
            early = jnp.concatenate([saved[1][1], dpre_saved[1], saved[0][1]], axis=1)
            early_all = lax.all_gather(early, "dp", tiled=True)
            upper, early_all = lax.optimization_barrier((upper, early_all))

    rows = width // data_groups
    late_all = lax.all_gather(dpre_saved[0], "dp", tiled=True)
    act_rows = jnp.stack([
        lax.dynamic_slice_in_dim(early_all, 2 * width + group * rows, rows, axis=1),
        lax.dynamic_slice_in_dim(early_all, group * rows, rows, axis=1),
    ])
    dpre_all = jnp.stack([late_all, early_all[:, width:2 * width]])
    grads = lax.dot_general(
        act_rows, dpre_all, (((1,), (1,)), ((0,), (0,))), preferred_element_type=jnp.float32
    ).astype(jnp.bfloat16)
    return grads[:, None]


def solution(mesh):
    return jax.shard_map(
        on_device,
        mesh=mesh,
        in_specs=(
            P(("groups", "dp"), None),
            P(("groups", "dp"), None),
            P(("groups", "dp"), None),
            P(None, "segment", None, None),
            P(None, "segment", None),
        ),
        out_specs=P("groups", "segment", "dp", None),
        check_vma=False,
    )
```

```python
import math

import jax
import jax.numpy as jnp
from jax import lax
from jax.experimental import pallas as pl
from jax.experimental.pallas import tpu as pltpu
from jax.sharding import PartitionSpec as P

ROWS = 8


EPSILON = 1e-06


def mixing_blocks(neighbour_rows):
    positions = jnp.arange(neighbour_rows.shape[1], dtype=jnp.int32)
    matches = (neighbour_rows[:, :, :, None] == positions[None, None, None, :]).astype(jnp.float32)
    return jnp.sum(matches, axis=2) * (0.5 / neighbour_rows.shape[2])


def mix_apply(mixing, values):
    micro = mixing.shape[0]
    blocks = values.reshape(micro, ROWS, values.shape[-1])
    mixed = jnp.einsum("bik,bkd->bid", mixing, blocks, precision=lax.Precision.HIGHEST)
    return mixed.reshape(values.shape)


def mix_apply_t(mixing, values):
    micro = mixing.shape[0]
    blocks = values.reshape(micro, ROWS, values.shape[-1])
    mixed = jnp.einsum("bki,bkd->bid", mixing, blocks, precision=lax.Precision.HIGHEST)
    return mixed.reshape(values.shape)


def layer_forward(residual, weight, gain_row, mixing):
    widened = residual.astype(jnp.float32)
    inverse = lax.rsqrt(jnp.mean(widened * widened, axis=-1, keepdims=True) + EPSILON)
    normed = widened * inverse * gain_row
    blended = 0.5 * normed + mix_apply(mixing, normed)
    active = blended.astype(jnp.bfloat16)
    before = jnp.dot(active, weight, preferred_element_type=jnp.float32)
    squashed = jnp.tanh(before)
    return ((widened + squashed).astype(jnp.bfloat16), active, squashed, inverse)


def layer_backward(residual, squashed, inverse, weight, gain_row, mixing, upper_grad):
    widened = residual.astype(jnp.float32)
    above = upper_grad.astype(jnp.float32)
    dbefore = (above * (1.0 - squashed * squashed)).astype(jnp.bfloat16)
    dblend = lax.dot_general(
        dbefore, weight, (((1,), (1,)), ((), ())), preferred_element_type=jnp.float32
    )
    dnormed = (0.5 * dblend + mix_apply_t(mixing, dblend)) * gain_row
    inner_mean = jnp.mean(dnormed * widened, axis=-1, keepdims=True)
    lower_grad = above + inverse * dnormed - widened * (inverse * inverse * inverse) * inner_mean
    return (lower_grad.astype(jnp.bfloat16), dbefore)


def fetch_kernel(phase, weights_hbm, after_hbm, out_vmem, sem):
    del after_hbm
    copy = pltpu.make_async_copy(weights_hbm.at[phase, 0], out_vmem, sem)
    copy.start()
    copy.wait()


def resident_weight(weights, phase, after):
    width = weights.shape[-1]
    return pl.pallas_call(
        lambda *refs: fetch_kernel(phase, *refs),
        in_specs=[pl.BlockSpec(memory_space=pl.ANY), pl.BlockSpec(memory_space=pl.ANY)],
        out_specs=pl.BlockSpec(memory_space=pltpu.VMEM),
        out_shape=jax.ShapeDtypeStruct((width, width), weights.dtype),
        scratch_shapes=[pltpu.SemaphoreType.DMA(())],
    )(weights, after)


def hop(array, source, target):
    return lax.ppermute(array, "segment", [(source, target)])


def on_device(fields, targets, neighbours, weights, gains):
    segments = lax.axis_size("segment")
    data_groups = lax.axis_size("dp")
    place = lax.axis_index("segment")
    group = lax.axis_index("dp")
    tokens, width = fields.shape
    micro_count = tokens // ROWS
    scale_top = 1.0 / math.sqrt(tokens * data_groups)
    mixing = mixing_blocks(neighbours.reshape(micro_count, ROWS, neighbours.shape[1]))
    weight_pair = [weights[0, 0], None]
    gain_pair = gains[:, 0]
    layer_count = 2 * segments

    state = fields
    saved = [None, None]
    for layer in range(layer_count):
        phase, member = divmod(layer, segments)
        result, active, squashed, inverse = layer_forward(
            state, weight_pair[phase], gain_pair[phase], mixing
        )
        if layer == 0:
            weight_pair = [resident_weight(weights, phase, result) for phase in range(2)]
        values = (state, active, squashed, inverse)
        if member == 0:
            saved[phase] = values
        else:
            mine = place == member
            saved[phase] = tuple(jnp.where(mine, new, old) for new, old in zip(values, saved[phase]))
        if layer + 1 < layer_count:
            state = hop(result, layer % segments, (layer + 1) % segments)
        else:
            state = result
        if layer == 0:
            state, weight_pair[1] = lax.optimization_barrier((state, weight_pair[1]))

    upper = ((state.astype(jnp.float32) - targets.astype(jnp.float32)) * scale_top).astype(jnp.bfloat16)

    dpre_saved = [None, None]
    for layer in reversed(range(layer_count)):
        phase, member = divmod(layer, segments)
        residual, _, squashed, inverse = saved[phase]
        lower, dbefore = layer_backward(
            residual, squashed, inverse, weight_pair[phase], gain_pair[phase], mixing, upper
        )
        if member == segments - 1:
            dpre_saved[phase] = dbefore
        else:
            dpre_saved[phase] = jnp.where(place == member, dbefore, dpre_saved[phase])
        if layer > 0:
            upper = hop(lower, layer % segments, (layer - 1) % segments)
        if layer == segments:
            early = jnp.concatenate([saved[1][1], dpre_saved[1], saved[0][1]], axis=1)
            early_all = lax.all_gather(early, "dp", tiled=True)
            upper, early_all = lax.optimization_barrier((upper, early_all))

    rows = width // data_groups
    late_all = lax.all_gather(dpre_saved[0], "dp", tiled=True)
    act_rows = jnp.stack([
        lax.dynamic_slice_in_dim(early_all, 2 * width + group * rows, rows, axis=1),
        lax.dynamic_slice_in_dim(early_all, group * rows, rows, axis=1),
    ])
    dpre_all = jnp.stack([late_all, early_all[:, width:2 * width]])
    grads = lax.dot_general(
        act_rows, dpre_all, (((1,), (1,)), ((0,), (0,))), preferred_element_type=jnp.float32
    ).astype(jnp.bfloat16)
    return grads[:, None]


def solution(mesh):
    return jax.shard_map(
        on_device,
        mesh=mesh,
        in_specs=(
            P(("groups", "dp"), None),
            P(("groups", "dp"), None),
            P(("groups", "dp"), None),
            P(None, "segment", None, None),
            P(None, "segment", None),
        ),
        out_specs=P("groups", "segment", "dp", None),
        check_vma=False,
    )
```

```python
import math

import jax
import jax.numpy as jnp
from jax import lax
from jax.experimental import pallas as pl
from jax.experimental.pallas import tpu as pltpu
from jax.sharding import PartitionSpec as P

ROWS = 8


EPSILON = 1e-06


def mixing_blocks(neighbour_rows):
    positions = jnp.arange(neighbour_rows.shape[1], dtype=jnp.int32)
    matches = (neighbour_rows[:, :, :, None] == positions[None, None, None, :]).astype(jnp.float32)
    return jnp.sum(matches, axis=2) * (0.5 / neighbour_rows.shape[2])


def mix_apply(mixing, values):
    micro = mixing.shape[0]
    blocks = values.reshape(micro, ROWS, values.shape[-1])
    mixed = jnp.einsum("bik,bkd->bid", mixing, blocks, precision=lax.Precision.HIGHEST)
    return mixed.reshape(values.shape)


def mix_apply_t(mixing, values):
    micro = mixing.shape[0]
    blocks = values.reshape(micro, ROWS, values.shape[-1])
    mixed = jnp.einsum("bki,bkd->bid", mixing, blocks, precision=lax.Precision.HIGHEST)
    return mixed.reshape(values.shape)


def layer_forward(residual, weight, gain_row, mixing):
    widened = residual.astype(jnp.float32)
    inverse = lax.rsqrt(jnp.mean(widened * widened, axis=-1, keepdims=True) + EPSILON)
    normed = widened * inverse * gain_row
    blended = 0.5 * normed + mix_apply(mixing, normed)
    active = blended.astype(jnp.bfloat16)
    before = jnp.dot(active, weight, preferred_element_type=jnp.float32)
    squashed = jnp.tanh(before)
    return ((widened + squashed).astype(jnp.bfloat16), active, squashed, inverse)


def layer_backward(residual, squashed, inverse, weight, gain_row, mixing, upper_grad):
    widened = residual.astype(jnp.float32)
    above = upper_grad.astype(jnp.float32)
    dbefore = (above * (1.0 - squashed * squashed)).astype(jnp.bfloat16)
    dblend = lax.dot_general(
        dbefore, weight, (((1,), (1,)), ((), ())), preferred_element_type=jnp.float32
    )
    dnormed = (0.5 * dblend + mix_apply_t(mixing, dblend)) * gain_row
    inner_mean = jnp.mean(dnormed * widened, axis=-1, keepdims=True)
    lower_grad = above + inverse * dnormed - widened * (inverse * inverse * inverse) * inner_mean
    return (lower_grad.astype(jnp.bfloat16), dbefore)


def fetch_kernel(phase, weights_hbm, out_vmem, sem):
    copy = pltpu.make_async_copy(weights_hbm.at[phase, 0], out_vmem, sem)
    copy.start()
    copy.wait()


def resident_weight(weights, phase):
    width = weights.shape[-1]
    return pl.pallas_call(
        lambda *refs: fetch_kernel(phase, *refs),
        in_specs=[pl.BlockSpec(memory_space=pl.ANY)],
        out_specs=pl.BlockSpec(memory_space=pltpu.VMEM),
        out_shape=jax.ShapeDtypeStruct((width, width), weights.dtype),
        scratch_shapes=[pltpu.SemaphoreType.DMA(())],
    )(weights)


def hop(array, source, target):
    return lax.ppermute(array, "segment", [(source, target)])


def on_device(fields, targets, neighbours, weights, gains):
    segments = lax.axis_size("segment")
    data_groups = lax.axis_size("dp")
    place = lax.axis_index("segment")
    group = lax.axis_index("dp")
    tokens, width = fields.shape
    micro_count = tokens // ROWS
    scale_top = 1.0 / math.sqrt(tokens * data_groups)
    mixing = mixing_blocks(neighbours.reshape(micro_count, ROWS, neighbours.shape[1]))
    weight_pair = [resident_weight(weights, phase) for phase in range(2)]
    gain_pair = gains[:, 0]
    layer_count = 2 * segments
    last = segments - 1

    core = group % 2
    half = width // 2
    own_half = lax.dynamic_slice_in_dim(weights[0, 0], core * half, half, axis=0)
    came = lax.ppermute(own_half, "segment", [(last, 0)])
    other = lax.ppermute(came, "dp", [(g, g ^ 1) for g in range(data_groups)])
    low_half = jnp.where(core == 0, came, other)
    high_half = jnp.where(core == 0, other, came)
    moved_weight = jnp.concatenate([low_half, high_half], axis=0)
    moved_gain = lax.ppermute(gains[0, 0], "segment", [(last, 0)])

    state = fields
    saved = [None, None]
    for layer in range(layer_count):
        phase, member = divmod(layer, segments)
        result, active, squashed, inverse = layer_forward(
            state, weight_pair[phase], gain_pair[phase], mixing
        )
        values = (state, active, squashed, inverse)
        if member == 0:
            saved[phase] = values
        else:
            mine = place == member
            saved[phase] = tuple(jnp.where(mine, new, old) for new, old in zip(values, saved[phase]))
        if layer + 1 < layer_count:
            state = hop(result, layer % segments, (layer + 1) % segments)
        else:
            state = result

    moved_state = lax.ppermute(saved[0][0], "segment", [(last, 0)])
    moved_squashed = lax.ppermute(saved[0][2], "segment", [(last, 0)])

    upper = ((state.astype(jnp.float32) - targets.astype(jnp.float32)) * scale_top).astype(jnp.bfloat16)

    def runs_on(layer):
        return 0 if layer == last else layer % segments

    dpre_saved = [None, None]
    moved_dpre = None
    for layer in reversed(range(layer_count)):
        phase, member = divmod(layer, segments)
        if layer == last:
            residual, squashed = moved_state, moved_squashed
            widened = residual.astype(jnp.float32)
            inverse = lax.rsqrt(jnp.mean(widened * widened, axis=-1, keepdims=True) + EPSILON)
            weight, gain = moved_weight, moved_gain
        else:
            residual, _, squashed, inverse = saved[phase]
            weight, gain = weight_pair[phase], gain_pair[phase]
        lower, dbefore = layer_backward(residual, squashed, inverse, weight, gain, mixing, upper)
        if layer == last:
            moved_dpre = dbefore
        elif member == segments - 1 or (phase == 0 and member == segments - 2):
            dpre_saved[phase] = dbefore
        else:
            dpre_saved[phase] = jnp.where(place == member, dbefore, dpre_saved[phase])
        if layer > 0:
            source, target = runs_on(layer), runs_on(layer - 1)
            upper = lower if source == target else hop(lower, source, target)

    returned = lax.ppermute(moved_dpre, "segment", [(0, last)])
    dpre_first = jnp.where(place == last, returned, dpre_saved[0])

    rows = width // data_groups
    early = jnp.concatenate([saved[1][1], dpre_saved[1], saved[0][1]], axis=1)
    early_all = lax.all_gather(early, "dp", tiled=True)
    late_all = lax.all_gather(dpre_first, "dp", tiled=True)
    act_rows = jnp.stack([
        lax.dynamic_slice_in_dim(early_all, 2 * width + group * rows, rows, axis=1),
        lax.dynamic_slice_in_dim(early_all, group * rows, rows, axis=1),
    ])
    dpre_all = jnp.stack([late_all, early_all[:, width:2 * width]])
    grads = lax.dot_general(
        act_rows, dpre_all, (((1,), (1,)), ((0,), (0,))), preferred_element_type=jnp.float32
    ).astype(jnp.bfloat16)
    return grads[:, None]


def solution(mesh):
    return jax.shard_map(
        on_device,
        mesh=mesh,
        in_specs=(
            P(("groups", "dp"), None),
            P(("groups", "dp"), None),
            P(("groups", "dp"), None),
            P(None, "segment", None, None),
            P(None, "segment", None),
        ),
        out_specs=P("groups", "segment", "dp", None),
        check_vma=False,
    )
```

```python
import math

import jax
import jax.numpy as jnp
from jax import lax
from jax.experimental import pallas as pl
from jax.experimental.pallas import tpu as pltpu
from jax.sharding import PartitionSpec as P

ROWS = 8


EPSILON = 1e-06


def mixing_blocks(neighbour_rows):
    positions = jnp.arange(neighbour_rows.shape[1], dtype=jnp.int32)
    matches = (neighbour_rows[:, :, :, None] == positions[None, None, None, :]).astype(jnp.float32)
    return jnp.sum(matches, axis=2) * (0.5 / neighbour_rows.shape[2])


def mix_apply(mixing, values):
    micro = mixing.shape[0]
    blocks = values.reshape(micro, ROWS, values.shape[-1])
    mixed = jnp.einsum("bik,bkd->bid", mixing, blocks, precision=lax.Precision.HIGHEST)
    return mixed.reshape(values.shape)


def mix_apply_t(mixing, values):
    micro = mixing.shape[0]
    blocks = values.reshape(micro, ROWS, values.shape[-1])
    mixed = jnp.einsum("bki,bkd->bid", mixing, blocks, precision=lax.Precision.HIGHEST)
    return mixed.reshape(values.shape)


def layer_forward(residual, weight, gain_row, mixing):
    widened = residual.astype(jnp.float32)
    inverse = lax.rsqrt(jnp.mean(widened * widened, axis=-1, keepdims=True) + EPSILON)
    normed = widened * inverse * gain_row
    blended = 0.5 * normed + mix_apply(mixing, normed)
    active = blended.astype(jnp.bfloat16)
    before = jnp.dot(active, weight, preferred_element_type=jnp.float32)
    squashed = jnp.tanh(before)
    return ((widened + squashed).astype(jnp.bfloat16), active, squashed, inverse)


def layer_backward(residual, squashed, inverse, weight, gain_row, mixing, upper_grad):
    widened = residual.astype(jnp.float32)
    above = upper_grad.astype(jnp.float32)
    dbefore = (above * (1.0 - squashed * squashed)).astype(jnp.bfloat16)
    dblend = lax.dot_general(
        dbefore, weight, (((1,), (1,)), ((), ())), preferred_element_type=jnp.float32
    )
    dnormed = (0.5 * dblend + mix_apply_t(mixing, dblend)) * gain_row
    inner_mean = jnp.mean(dnormed * widened, axis=-1, keepdims=True)
    lower_grad = above + inverse * dnormed - widened * (inverse * inverse * inverse) * inner_mean
    return (lower_grad.astype(jnp.bfloat16), dbefore)


def fetch_kernel(phase, weights_hbm, out_vmem, sem):
    copy = pltpu.make_async_copy(weights_hbm.at[phase, 0], out_vmem, sem)
    copy.start()
    copy.wait()


def resident_weight(weights, phase):
    width = weights.shape[-1]
    return pl.pallas_call(
        lambda *refs: fetch_kernel(phase, *refs),
        in_specs=[pl.BlockSpec(memory_space=pl.ANY)],
        out_specs=pl.BlockSpec(memory_space=pltpu.VMEM),
        out_shape=jax.ShapeDtypeStruct((width, width), weights.dtype),
        scratch_shapes=[pltpu.SemaphoreType.DMA(())],
    )(weights)


def hop(array, source, target):
    return lax.ppermute(array, "segment", [(source, target)])


def on_device(fields, targets, neighbours, weights, gains):
    segments = lax.axis_size("segment")
    data_groups = lax.axis_size("dp")
    place = lax.axis_index("segment")
    group = lax.axis_index("dp")
    tokens, width = fields.shape
    micro_count = tokens // ROWS
    scale_top = 1.0 / math.sqrt(tokens * data_groups)
    mixing = mixing_blocks(neighbours.reshape(micro_count, ROWS, neighbours.shape[1]))
    weight_pair = [resident_weight(weights, phase) for phase in range(2)]
    gain_pair = gains[:, 0]
    layer_count = 2 * segments

    state = fields
    saved = [None, None]
    for layer in range(layer_count):
        phase, member = divmod(layer, segments)
        if layer == 0:
            def skip(*_):
                return (
                    jnp.zeros_like(state), jnp.zeros_like(state),
                    jnp.zeros(state.shape, jnp.float32), jnp.zeros((tokens, 1), jnp.float32),
                )

            result, active, squashed, inverse = lax.cond(
                place == 0, layer_forward, skip,
                state, weight_pair[phase], gain_pair[phase], mixing,
            )
        else:
            result, active, squashed, inverse = layer_forward(
                state, weight_pair[phase], gain_pair[phase], mixing
            )
        values = (state, active, squashed, inverse)
        if member == 0:
            saved[phase] = values
        else:
            mine = place == member
            saved[phase] = tuple(jnp.where(mine, new, old) for new, old in zip(values, saved[phase]))
        if layer + 1 < layer_count:
            state = hop(result, layer % segments, (layer + 1) % segments)
        else:
            state = result

    upper = ((state.astype(jnp.float32) - targets.astype(jnp.float32)) * scale_top).astype(jnp.bfloat16)

    dpre_saved = [None, None]
    for layer in reversed(range(layer_count)):
        phase, member = divmod(layer, segments)
        residual, _, squashed, inverse = saved[phase]
        lower, dbefore = layer_backward(
            residual, squashed, inverse, weight_pair[phase], gain_pair[phase], mixing, upper
        )
        if member == segments - 1:
            dpre_saved[phase] = dbefore
        else:
            dpre_saved[phase] = jnp.where(place == member, dbefore, dpre_saved[phase])
        if layer > 0:
            upper = hop(lower, layer % segments, (layer - 1) % segments)
        if layer == segments:
            early = jnp.concatenate([saved[1][1], dpre_saved[1], saved[0][1]], axis=1)
            early_all = lax.all_gather(early, "dp", tiled=True)
            upper, early_all = lax.optimization_barrier((upper, early_all))

    rows = width // data_groups
    late_all = lax.all_gather(dpre_saved[0], "dp", tiled=True)
    act_rows = jnp.stack([
        lax.dynamic_slice_in_dim(early_all, 2 * width + group * rows, rows, axis=1),
        lax.dynamic_slice_in_dim(early_all, group * rows, rows, axis=1),
    ])
    dpre_all = jnp.stack([late_all, early_all[:, width:2 * width]])
    grads = lax.dot_general(
        act_rows, dpre_all, (((1,), (1,)), ((0,), (0,))), preferred_element_type=jnp.float32
    ).astype(jnp.bfloat16)
    return grads[:, None]


def solution(mesh):
    return jax.shard_map(
        on_device,
        mesh=mesh,
        in_specs=(
            P(("groups", "dp"), None),
            P(("groups", "dp"), None),
            P(("groups", "dp"), None),
            P(None, "segment", None, None),
            P(None, "segment", None),
        ),
        out_specs=P("groups", "segment", "dp", None),
        check_vma=False,
    )
```

```python
import math

import jax
import jax.numpy as jnp
from jax import lax
from jax.experimental import pallas as pl
from jax.experimental.pallas import tpu as pltpu
from jax.sharding import PartitionSpec as P

ROWS = 8


EPSILON = 1e-06


def mixing_blocks(neighbour_rows):
    positions = jnp.arange(neighbour_rows.shape[1], dtype=jnp.int32)
    matches = (neighbour_rows[:, :, :, None] == positions[None, None, None, :]).astype(jnp.float32)
    return jnp.sum(matches, axis=2) * (0.5 / neighbour_rows.shape[2])


def mix_apply(mixing, values):
    micro = mixing.shape[0]
    blocks = values.reshape(micro, ROWS, values.shape[-1])
    mixed = jnp.einsum("bik,bkd->bid", mixing, blocks, precision=lax.Precision.HIGHEST)
    return mixed.reshape(values.shape)


def mix_apply_t(mixing, values):
    micro = mixing.shape[0]
    blocks = values.reshape(micro, ROWS, values.shape[-1])
    mixed = jnp.einsum("bki,bkd->bid", mixing, blocks, precision=lax.Precision.HIGHEST)
    return mixed.reshape(values.shape)


def layer_forward(residual, weight, gain_row, mixing):
    widened = residual.astype(jnp.float32)
    inverse = lax.rsqrt(jnp.mean(widened * widened, axis=-1, keepdims=True) + EPSILON)
    normed = widened * inverse * gain_row
    blended = 0.5 * normed + mix_apply(mixing, normed)
    active = blended.astype(jnp.bfloat16)
    before = jnp.dot(active, weight, preferred_element_type=jnp.float32)
    squashed = jnp.tanh(before)
    return ((widened + squashed).astype(jnp.bfloat16), active, squashed, inverse)


def layer_backward(residual, squashed, inverse, weight, gain_row, mixing, upper_grad):
    widened = residual.astype(jnp.float32)
    above = upper_grad.astype(jnp.float32)
    dbefore = (above * (1.0 - squashed * squashed)).astype(jnp.bfloat16)
    dblend = lax.dot_general(
        dbefore, weight, (((1,), (1,)), ((), ())), preferred_element_type=jnp.float32
    )
    dnormed = (0.5 * dblend + mix_apply_t(mixing, dblend)) * gain_row
    inner_mean = jnp.mean(dnormed * widened, axis=-1, keepdims=True)
    lower_grad = above + inverse * dnormed - widened * (inverse * inverse * inverse) * inner_mean
    return (lower_grad.astype(jnp.bfloat16), dbefore)


def fetch_kernel(phase, weights_hbm, out_vmem, sem):
    copy = pltpu.make_async_copy(weights_hbm.at[phase, 0], out_vmem, sem)
    copy.start()
    copy.wait()


def resident_weight(weights, phase):
    width = weights.shape[-1]
    return pl.pallas_call(
        lambda *refs: fetch_kernel(phase, *refs),
        in_specs=[pl.BlockSpec(memory_space=pl.ANY)],
        out_specs=pl.BlockSpec(memory_space=pltpu.VMEM),
        out_shape=jax.ShapeDtypeStruct((width, width), weights.dtype),
        scratch_shapes=[pltpu.SemaphoreType.DMA(())],
    )(weights)


def hop(array, source, target):
    return lax.ppermute(array, "segment", [(source, target)])


def on_device(fields, targets, neighbours, weights, gains):
    segments = lax.axis_size("segment")
    data_groups = lax.axis_size("dp")
    place = lax.axis_index("segment")
    group = lax.axis_index("dp")
    tokens, width = fields.shape
    micro_count = tokens // ROWS
    scale_top = 1.0 / math.sqrt(tokens * data_groups)
    mixing = mixing_blocks(neighbours.reshape(micro_count, ROWS, neighbours.shape[1]))
    weight_pair = [resident_weight(weights, phase) for phase in range(2)]
    gain_pair = gains[:, 0]
    layer_count = 2 * segments

    def forward_skip(state, *_):
        return (
            jnp.zeros_like(state), jnp.zeros_like(state),
            jnp.zeros(state.shape, jnp.float32), jnp.zeros((tokens, 1), jnp.float32),
        )

    def backward_skip(residual, *_):
        return (jnp.zeros_like(residual), jnp.zeros_like(residual))

    state = fields
    saved = [None, None]
    for layer in range(layer_count):
        phase, member = divmod(layer, segments)
        if layer == 0:
            result, active, squashed, inverse = lax.cond(
                place == member, layer_forward, forward_skip,
                state, weight_pair[phase], gain_pair[phase], mixing,
            )
        else:
            result, active, squashed, inverse = layer_forward(
                state, weight_pair[phase], gain_pair[phase], mixing
            )
        values = (state, active, squashed, inverse)
        if member == 0:
            saved[phase] = values
        else:
            mine = place == member
            saved[phase] = tuple(jnp.where(mine, new, old) for new, old in zip(values, saved[phase]))
        if layer + 1 < layer_count:
            state = hop(result, layer % segments, (layer + 1) % segments)
        else:
            state = result

    upper = ((state.astype(jnp.float32) - targets.astype(jnp.float32)) * scale_top).astype(jnp.bfloat16)

    dpre_saved = [None, None]
    for layer in reversed(range(layer_count)):
        phase, member = divmod(layer, segments)
        residual, _, squashed, inverse = saved[phase]
        lower, dbefore = lax.cond(
            place == member, layer_backward, backward_skip,
            residual, squashed, inverse, weight_pair[phase], gain_pair[phase], mixing, upper,
        )
        if member == segments - 1:
            dpre_saved[phase] = dbefore
        else:
            dpre_saved[phase] = jnp.where(place == member, dbefore, dpre_saved[phase])
        if layer > 0:
            upper = hop(lower, layer % segments, (layer - 1) % segments)
        if layer == segments:
            early = jnp.concatenate([saved[1][1], dpre_saved[1], saved[0][1]], axis=1)
            early_all = lax.all_gather(early, "dp", tiled=True)
            upper, early_all = lax.optimization_barrier((upper, early_all))

    rows = width // data_groups
    late_all = lax.all_gather(dpre_saved[0], "dp", tiled=True)
    act_rows = jnp.stack([
        lax.dynamic_slice_in_dim(early_all, 2 * width + group * rows, rows, axis=1),
        lax.dynamic_slice_in_dim(early_all, group * rows, rows, axis=1),
    ])
    dpre_all = jnp.stack([late_all, early_all[:, width:2 * width]])
    grads = lax.dot_general(
        act_rows, dpre_all, (((1,), (1,)), ((0,), (0,))), preferred_element_type=jnp.float32
    ).astype(jnp.bfloat16)
    return grads[:, None]


def solution(mesh):
    return jax.shard_map(
        on_device,
        mesh=mesh,
        in_specs=(
            P(("groups", "dp"), None),
            P(("groups", "dp"), None),
            P(("groups", "dp"), None),
            P(None, "segment", None, None),
            P(None, "segment", None),
        ),
        out_specs=P("groups", "segment", "dp", None),
        check_vma=False,
    )
```

```python
import math

import jax
import jax.numpy as jnp
from jax import lax
from jax.experimental import pallas as pl
from jax.experimental.pallas import tpu as pltpu
from jax.sharding import PartitionSpec as P

ROWS = 8


EPSILON = 1e-06


def mixing_blocks(neighbour_rows):
    positions = jnp.arange(neighbour_rows.shape[1], dtype=jnp.int32)
    matches = (neighbour_rows[:, :, :, None] == positions[None, None, None, :]).astype(jnp.float32)
    return jnp.sum(matches, axis=2) * (0.5 / neighbour_rows.shape[2])


def mix_apply(mixing, values):
    micro = mixing.shape[0]
    blocks = values.reshape(micro, ROWS, values.shape[-1])
    mixed = jnp.einsum("bik,bkd->bid", mixing, blocks, precision=lax.Precision.HIGHEST)
    return mixed.reshape(values.shape)


def mix_apply_t(mixing, values):
    micro = mixing.shape[0]
    blocks = values.reshape(micro, ROWS, values.shape[-1])
    mixed = jnp.einsum("bki,bkd->bid", mixing, blocks, precision=lax.Precision.HIGHEST)
    return mixed.reshape(values.shape)


def layer_forward(residual, weight, gain_row, mixing):
    widened = residual.astype(jnp.float32)
    inverse = lax.rsqrt(jnp.mean(widened * widened, axis=-1, keepdims=True) + EPSILON)
    normed = widened * inverse * gain_row
    blended = 0.5 * normed + mix_apply(mixing, normed)
    active = blended.astype(jnp.bfloat16)
    before = jnp.dot(active, weight, preferred_element_type=jnp.float32)
    squashed = jnp.tanh(before)
    return ((widened + squashed).astype(jnp.bfloat16), active, squashed, inverse)


def layer_backward(residual, squashed, inverse, weight, gain_row, mixing, upper_grad):
    widened = residual.astype(jnp.float32)
    above = upper_grad.astype(jnp.float32)
    dbefore = (above * (1.0 - squashed * squashed)).astype(jnp.bfloat16)
    dblend = lax.dot_general(
        dbefore, weight, (((1,), (1,)), ((), ())), preferred_element_type=jnp.float32
    )
    dnormed = (0.5 * dblend + mix_apply_t(mixing, dblend)) * gain_row
    inner_mean = jnp.mean(dnormed * widened, axis=-1, keepdims=True)
    lower_grad = above + inverse * dnormed - widened * (inverse * inverse * inverse) * inner_mean
    return (lower_grad.astype(jnp.bfloat16), dbefore)


def fetch_kernel(phase, weights_hbm, out_vmem, sem):
    copy = pltpu.make_async_copy(weights_hbm.at[phase, 0], out_vmem, sem)
    copy.start()
    copy.wait()


def resident_weight(weights, phase):
    width = weights.shape[-1]
    return pl.pallas_call(
        lambda *refs: fetch_kernel(phase, *refs),
        in_specs=[pl.BlockSpec(memory_space=pl.ANY)],
        out_specs=pl.BlockSpec(memory_space=pltpu.VMEM),
        out_shape=jax.ShapeDtypeStruct((width, width), weights.dtype),
        scratch_shapes=[pltpu.SemaphoreType.DMA(())],
    )(weights)


def hop(array, source, target):
    return lax.ppermute(array, "segment", [(source, target)])


def on_device(fields, targets, neighbours, weights, gains):
    segments = lax.axis_size("segment")
    data_groups = lax.axis_size("dp")
    place = lax.axis_index("segment")
    group = lax.axis_index("dp")
    tokens, width = fields.shape
    micro_count = tokens // ROWS
    scale_top = 1.0 / math.sqrt(tokens * data_groups)
    mixing = mixing_blocks(neighbours.reshape(micro_count, ROWS, neighbours.shape[1]))
    weight_pair = [resident_weight(weights, phase) for phase in range(2)]
    gain_pair = gains[:, 0]
    layer_count = 2 * segments

    state = fields
    saved = [None, None]
    for layer in range(layer_count):
        phase, member = divmod(layer, segments)
        if member == 0:
            def skip(*_):
                return (
                    jnp.zeros_like(state), jnp.zeros_like(state),
                    jnp.zeros(state.shape, jnp.float32), jnp.zeros((tokens, 1), jnp.float32),
                )

            result, active, squashed, inverse = lax.cond(
                place == 0, layer_forward, skip,
                state, weight_pair[phase], gain_pair[phase], mixing,
            )
        else:
            result, active, squashed, inverse = layer_forward(
                state, weight_pair[phase], gain_pair[phase], mixing
            )
        values = (state, active, squashed, inverse)
        if member == 0:
            saved[phase] = values
        else:
            mine = place == member
            saved[phase] = tuple(jnp.where(mine, new, old) for new, old in zip(values, saved[phase]))
        if layer + 1 < layer_count:
            state = hop(result, layer % segments, (layer + 1) % segments)
        else:
            state = result

    upper = ((state.astype(jnp.float32) - targets.astype(jnp.float32)) * scale_top).astype(jnp.bfloat16)

    dpre_saved = [None, None]
    for layer in reversed(range(layer_count)):
        phase, member = divmod(layer, segments)
        residual, _, squashed, inverse = saved[phase]
        lower, dbefore = layer_backward(
            residual, squashed, inverse, weight_pair[phase], gain_pair[phase], mixing, upper
        )
        if member == segments - 1:
            dpre_saved[phase] = dbefore
        else:
            dpre_saved[phase] = jnp.where(place == member, dbefore, dpre_saved[phase])
        if layer > 0:
            upper = hop(lower, layer % segments, (layer - 1) % segments)
        if layer == segments:
            early = jnp.concatenate([saved[1][1], dpre_saved[1], saved[0][1]], axis=1)
            early_all = lax.all_gather(early, "dp", tiled=True)
            upper, early_all = lax.optimization_barrier((upper, early_all))

    rows = width // data_groups
    late_all = lax.all_gather(dpre_saved[0], "dp", tiled=True)
    act_rows = jnp.stack([
        lax.dynamic_slice_in_dim(early_all, 2 * width + group * rows, rows, axis=1),
        lax.dynamic_slice_in_dim(early_all, group * rows, rows, axis=1),
    ])
    dpre_all = jnp.stack([late_all, early_all[:, width:2 * width]])
    grads = lax.dot_general(
        act_rows, dpre_all, (((1,), (1,)), ((0,), (0,))), preferred_element_type=jnp.float32
    ).astype(jnp.bfloat16)
    return grads[:, None]


def solution(mesh):
    return jax.shard_map(
        on_device,
        mesh=mesh,
        in_specs=(
            P(("groups", "dp"), None),
            P(("groups", "dp"), None),
            P(("groups", "dp"), None),
            P(None, "segment", None, None),
            P(None, "segment", None),
        ),
        out_specs=P("groups", "segment", "dp", None),
        check_vma=False,
    )
```

```python
import math

import jax
import jax.numpy as jnp
from jax import lax
from jax.experimental import pallas as pl
from jax.experimental.pallas import tpu as pltpu
from jax.sharding import PartitionSpec as P

ROWS = 8


EPSILON = 1e-06


def mixing_blocks(neighbour_rows):
    positions = jnp.arange(neighbour_rows.shape[1], dtype=jnp.int32)
    matches = (neighbour_rows[:, :, :, None] == positions[None, None, None, :]).astype(jnp.float32)
    return jnp.sum(matches, axis=2) * (0.5 / neighbour_rows.shape[2])


def mix_apply(mixing, values):
    micro = mixing.shape[0]
    blocks = values.reshape(micro, ROWS, values.shape[-1])
    mixed = jnp.einsum("bik,bkd->bid", mixing, blocks, precision=lax.Precision.HIGHEST)
    return mixed.reshape(values.shape)


def mix_apply_t(mixing, values):
    micro = mixing.shape[0]
    blocks = values.reshape(micro, ROWS, values.shape[-1])
    mixed = jnp.einsum("bki,bkd->bid", mixing, blocks, precision=lax.Precision.HIGHEST)
    return mixed.reshape(values.shape)


def layer_forward(residual, weight, gain_row, mixing):
    widened = residual.astype(jnp.float32)
    inverse = lax.rsqrt(jnp.mean(widened * widened, axis=-1, keepdims=True) + EPSILON)
    normed = widened * inverse * gain_row
    blended = 0.5 * normed + mix_apply(mixing, normed)
    active = blended.astype(jnp.bfloat16)
    before = jnp.dot(active, weight, preferred_element_type=jnp.float32)
    squashed = jnp.tanh(before)
    return ((widened + squashed).astype(jnp.bfloat16), active, squashed, inverse)


def layer_backward(residual, squashed, inverse, weight, gain_row, mixing, upper_grad):
    widened = residual.astype(jnp.float32)
    above = upper_grad.astype(jnp.float32)
    dbefore = (above * (1.0 - squashed * squashed)).astype(jnp.bfloat16)
    dblend = lax.dot_general(
        dbefore, weight, (((1,), (1,)), ((), ())), preferred_element_type=jnp.float32
    )
    dnormed = (0.5 * dblend + mix_apply_t(mixing, dblend)) * gain_row
    inner_mean = jnp.mean(dnormed * widened, axis=-1, keepdims=True)
    lower_grad = above + inverse * dnormed - widened * (inverse * inverse * inverse) * inner_mean
    return (lower_grad.astype(jnp.bfloat16), dbefore)


def fetch_kernel(phase, weights_hbm, out_vmem, sem):
    copy = pltpu.make_async_copy(weights_hbm.at[phase, 0], out_vmem, sem)
    copy.start()
    copy.wait()


def resident_weight(weights, phase):
    width = weights.shape[-1]
    return pl.pallas_call(
        lambda *refs: fetch_kernel(phase, *refs),
        in_specs=[pl.BlockSpec(memory_space=pl.ANY)],
        out_specs=pl.BlockSpec(memory_space=pltpu.VMEM),
        out_shape=jax.ShapeDtypeStruct((width, width), weights.dtype),
        scratch_shapes=[pltpu.SemaphoreType.DMA(())],
    )(weights)


def hop(array, source, target):
    return lax.ppermute(array, "segment", [(source, target)])


def on_device(fields, targets, neighbours, weights, gains):
    segments = lax.axis_size("segment")
    data_groups = lax.axis_size("dp")
    place = lax.axis_index("segment")
    group = lax.axis_index("dp")
    tokens, width = fields.shape
    micro_count = tokens // ROWS
    scale_top = 1.0 / math.sqrt(tokens * data_groups)
    mixing = mixing_blocks(neighbours.reshape(micro_count, ROWS, neighbours.shape[1]))
    weight_pair = [resident_weight(weights, phase) for phase in range(2)]
    gain_pair = gains[:, 0]
    layer_count = 2 * segments

    state = fields
    saved = [None, None]
    for layer in range(layer_count):
        phase, member = divmod(layer, segments)
        if layer in (0, layer_count - 1):
            def skip(*_):
                return (
                    jnp.zeros_like(state), jnp.zeros_like(state),
                    jnp.zeros(state.shape, jnp.float32), jnp.zeros((tokens, 1), jnp.float32),
                )

            result, active, squashed, inverse = lax.cond(
                place == member, layer_forward, skip,
                state, weight_pair[phase], gain_pair[phase], mixing,
            )
        else:
            result, active, squashed, inverse = layer_forward(
                state, weight_pair[phase], gain_pair[phase], mixing
            )
        values = (state, active, squashed, inverse)
        if member == 0:
            saved[phase] = values
        else:
            mine = place == member
            saved[phase] = tuple(jnp.where(mine, new, old) for new, old in zip(values, saved[phase]))
        if layer + 1 < layer_count:
            state = hop(result, layer % segments, (layer + 1) % segments)
        else:
            state = result

    upper = ((state.astype(jnp.float32) - targets.astype(jnp.float32)) * scale_top).astype(jnp.bfloat16)

    dpre_saved = [None, None]
    for layer in reversed(range(layer_count)):
        phase, member = divmod(layer, segments)
        residual, _, squashed, inverse = saved[phase]
        lower, dbefore = layer_backward(
            residual, squashed, inverse, weight_pair[phase], gain_pair[phase], mixing, upper
        )
        if member == segments - 1:
            dpre_saved[phase] = dbefore
        else:
            dpre_saved[phase] = jnp.where(place == member, dbefore, dpre_saved[phase])
        if layer > 0:
            upper = hop(lower, layer % segments, (layer - 1) % segments)
        if layer == segments:
            early = jnp.concatenate([saved[1][1], dpre_saved[1], saved[0][1]], axis=1)
            early_all = lax.all_gather(early, "dp", tiled=True)
            upper, early_all = lax.optimization_barrier((upper, early_all))

    rows = width // data_groups
    late_all = lax.all_gather(dpre_saved[0], "dp", tiled=True)
    act_rows = jnp.stack([
        lax.dynamic_slice_in_dim(early_all, 2 * width + group * rows, rows, axis=1),
        lax.dynamic_slice_in_dim(early_all, group * rows, rows, axis=1),
    ])
    dpre_all = jnp.stack([late_all, early_all[:, width:2 * width]])
    grads = lax.dot_general(
        act_rows, dpre_all, (((1,), (1,)), ((0,), (0,))), preferred_element_type=jnp.float32
    ).astype(jnp.bfloat16)
    return grads[:, None]


def solution(mesh):
    return jax.shard_map(
        on_device,
        mesh=mesh,
        in_specs=(
            P(("groups", "dp"), None),
            P(("groups", "dp"), None),
            P(("groups", "dp"), None),
            P(None, "segment", None, None),
            P(None, "segment", None),
        ),
        out_specs=P("groups", "segment", "dp", None),
        check_vma=False,
    )
```

```python
import math

import jax
import jax.numpy as jnp
from jax import lax
from jax.experimental import pallas as pl
from jax.experimental.pallas import tpu as pltpu
from jax.sharding import PartitionSpec as P

ROWS = 8


EPSILON = 1e-06


def mixing_full(neighbour_rows):
    tokens, count = neighbour_rows.shape
    row = lax.broadcasted_iota(jnp.int32, (tokens, tokens), 0)
    col = lax.broadcasted_iota(jnp.int32, (tokens, tokens), 1)
    base = row - row % ROWS
    hits = jnp.zeros((tokens, tokens), jnp.float32)
    for k in range(count):
        hits = hits + (neighbour_rows[:, k:k + 1] + base == col).astype(jnp.float32)
    return hits * (0.5 / count)


def mix_apply(mixing, values):
    return jnp.dot(mixing, values, precision=lax.Precision.HIGHEST)


def mix_apply_t(mixing, values):
    return lax.dot_general(
        mixing, values, (((0,), (0,)), ((), ())), precision=lax.Precision.HIGHEST
    )


def layer_forward(residual, weight, gain_row, mixing):
    widened = residual.astype(jnp.float32)
    inverse = lax.rsqrt(jnp.mean(widened * widened, axis=-1, keepdims=True) + EPSILON)
    normed = widened * inverse * gain_row
    blended = 0.5 * normed + mix_apply(mixing, normed)
    active = blended.astype(jnp.bfloat16)
    before = jnp.dot(active, weight, preferred_element_type=jnp.float32)
    squashed = jnp.tanh(before)
    return ((widened + squashed).astype(jnp.bfloat16), active, squashed, inverse)


def layer_backward(residual, squashed, inverse, weight, gain_row, mixing, upper_grad):
    widened = residual.astype(jnp.float32)
    above = upper_grad.astype(jnp.float32)
    dbefore = (above * (1.0 - squashed * squashed)).astype(jnp.bfloat16)
    dblend = lax.dot_general(
        dbefore, weight, (((1,), (1,)), ((), ())), preferred_element_type=jnp.float32
    )
    dnormed = (0.5 * dblend + mix_apply_t(mixing, dblend)) * gain_row
    inner_mean = jnp.mean(dnormed * widened, axis=-1, keepdims=True)
    lower_grad = above + inverse * dnormed - widened * (inverse * inverse * inverse) * inner_mean
    return (lower_grad.astype(jnp.bfloat16), dbefore)


def fetch_kernel(phase, weights_hbm, out_vmem, sem):
    copy = pltpu.make_async_copy(weights_hbm.at[phase, 0], out_vmem, sem)
    copy.start()
    copy.wait()


def resident_weight(weights, phase):
    width = weights.shape[-1]
    return pl.pallas_call(
        lambda *refs: fetch_kernel(phase, *refs),
        in_specs=[pl.BlockSpec(memory_space=pl.ANY)],
        out_specs=pl.BlockSpec(memory_space=pltpu.VMEM),
        out_shape=jax.ShapeDtypeStruct((width, width), weights.dtype),
        scratch_shapes=[pltpu.SemaphoreType.DMA(())],
    )(weights)


def hop(array, source, target):
    return lax.ppermute(array, "segment", [(source, target)])


def on_device(fields, targets, neighbours, weights, gains):
    segments = lax.axis_size("segment")
    data_groups = lax.axis_size("dp")
    place = lax.axis_index("segment")
    group = lax.axis_index("dp")
    tokens, width = fields.shape
    micro_count = tokens // ROWS
    scale_top = 1.0 / math.sqrt(tokens * data_groups)
    mixing = mixing_full(neighbours)
    weight_pair = [resident_weight(weights, phase) for phase in range(2)]
    gain_pair = gains[:, 0]
    layer_count = 2 * segments

    state = fields
    saved = [None, None]
    for layer in range(layer_count):
        phase, member = divmod(layer, segments)
        if layer == 0:
            def skip(*_):
                return (
                    jnp.zeros_like(state), jnp.zeros_like(state),
                    jnp.zeros(state.shape, jnp.float32), jnp.zeros((tokens, 1), jnp.float32),
                )

            result, active, squashed, inverse = lax.cond(
                place == 0, layer_forward, skip,
                state, weight_pair[phase], gain_pair[phase], mixing,
            )
        else:
            result, active, squashed, inverse = layer_forward(
                state, weight_pair[phase], gain_pair[phase], mixing
            )
        values = (state, active, squashed, inverse)
        if member == 0:
            saved[phase] = values
        else:
            mine = place == member
            saved[phase] = tuple(jnp.where(mine, new, old) for new, old in zip(values, saved[phase]))
        if layer + 1 < layer_count:
            state = hop(result, layer % segments, (layer + 1) % segments)
        else:
            state = result

    upper = ((state.astype(jnp.float32) - targets.astype(jnp.float32)) * scale_top).astype(jnp.bfloat16)

    dpre_saved = [None, None]
    for layer in reversed(range(layer_count)):
        phase, member = divmod(layer, segments)
        residual, _, squashed, inverse = saved[phase]
        lower, dbefore = layer_backward(
            residual, squashed, inverse, weight_pair[phase], gain_pair[phase], mixing, upper
        )
        if member == segments - 1:
            dpre_saved[phase] = dbefore
        else:
            dpre_saved[phase] = jnp.where(place == member, dbefore, dpre_saved[phase])
        if layer > 0:
            upper = hop(lower, layer % segments, (layer - 1) % segments)
        if layer == segments:
            early = jnp.concatenate([saved[1][1], dpre_saved[1], saved[0][1]], axis=1)
            early_all = lax.all_gather(early, "dp", tiled=True)
            upper, early_all = lax.optimization_barrier((upper, early_all))

    rows = width // data_groups
    late_all = lax.all_gather(dpre_saved[0], "dp", tiled=True)
    act_rows = jnp.stack([
        lax.dynamic_slice_in_dim(early_all, 2 * width + group * rows, rows, axis=1),
        lax.dynamic_slice_in_dim(early_all, group * rows, rows, axis=1),
    ])
    dpre_all = jnp.stack([late_all, early_all[:, width:2 * width]])
    grads = lax.dot_general(
        act_rows, dpre_all, (((1,), (1,)), ((0,), (0,))), preferred_element_type=jnp.float32
    ).astype(jnp.bfloat16)
    return grads[:, None]


def solution(mesh):
    return jax.shard_map(
        on_device,
        mesh=mesh,
        in_specs=(
            P(("groups", "dp"), None),
            P(("groups", "dp"), None),
            P(("groups", "dp"), None),
            P(None, "segment", None, None),
            P(None, "segment", None),
        ),
        out_specs=P("groups", "segment", "dp", None),
        check_vma=False,
    )
```

```python
import math

import jax
import jax.numpy as jnp
from jax import lax
from jax.experimental import pallas as pl
from jax.experimental.pallas import tpu as pltpu
from jax.sharding import PartitionSpec as P

ROWS = 8


EPSILON = 1e-06


def mixing_blocks(neighbour_rows):
    positions = jnp.arange(neighbour_rows.shape[1], dtype=jnp.int32)
    matches = (neighbour_rows[:, :, :, None] == positions[None, None, None, :]).astype(jnp.float32)
    return jnp.sum(matches, axis=2) * (0.5 / neighbour_rows.shape[2])


def mix_apply(mixing, values):
    micro = mixing.shape[0]
    blocks = values.reshape(micro, ROWS, values.shape[-1])
    mixed = jnp.einsum("bik,bkd->bid", mixing, blocks, precision=lax.Precision.HIGHEST)
    return mixed.reshape(values.shape)


def mix_apply_t(mixing, values):
    micro = mixing.shape[0]
    blocks = values.reshape(micro, ROWS, values.shape[-1])
    mixed = jnp.einsum("bki,bkd->bid", mixing, blocks, precision=lax.Precision.HIGHEST)
    return mixed.reshape(values.shape)


def layer_forward(residual, weight, gain_row, mixing):
    widened = residual.astype(jnp.float32)
    inverse = lax.rsqrt(jnp.mean(widened * widened, axis=-1, keepdims=True) + EPSILON)
    normed = widened * inverse * gain_row
    blended = 0.5 * normed + mix_apply(mixing, normed)
    active = blended.astype(jnp.bfloat16)
    before = jnp.dot(active, weight, preferred_element_type=jnp.float32)
    squashed = jnp.tanh(before)
    return ((widened + squashed).astype(jnp.bfloat16), active, squashed, inverse)


def layer_backward(residual, squashed, inverse, weight, gain_row, mixing, upper_grad):
    widened = residual.astype(jnp.float32)
    above = upper_grad.astype(jnp.float32)
    dbefore = (above * (1.0 - squashed * squashed)).astype(jnp.bfloat16)
    dblend = lax.dot_general(
        dbefore, weight, (((1,), (1,)), ((), ())), preferred_element_type=jnp.float32
    )
    dnormed = (0.5 * dblend + mix_apply_t(mixing, dblend)) * gain_row
    inner_mean = jnp.mean(dnormed * widened, axis=-1, keepdims=True)
    lower_grad = above + inverse * dnormed - widened * (inverse * inverse * inverse) * inner_mean
    return (lower_grad.astype(jnp.bfloat16), dbefore)


def fetch_kernel(phase, weights_hbm, out_vmem, sem):
    copy = pltpu.make_async_copy(weights_hbm.at[phase, 0], out_vmem, sem)
    copy.start()
    copy.wait()


def resident_weight(weights, phase):
    width = weights.shape[-1]
    return pl.pallas_call(
        lambda *refs: fetch_kernel(phase, *refs),
        in_specs=[pl.BlockSpec(memory_space=pl.ANY)],
        out_specs=pl.BlockSpec(memory_space=pltpu.VMEM),
        out_shape=jax.ShapeDtypeStruct((width, width), weights.dtype),
        scratch_shapes=[pltpu.SemaphoreType.DMA(())],
    )(weights)


def hop(array, source, target):
    return lax.ppermute(array, "segment", [(source, target)])


def on_device(fields, targets, neighbours, weights, gains):
    segments = lax.axis_size("segment")
    data_groups = lax.axis_size("dp")
    place = lax.axis_index("segment")
    group = lax.axis_index("dp")
    tokens, width = fields.shape
    micro_count = tokens // ROWS
    scale_top = 1.0 / math.sqrt(tokens * data_groups)
    mixing = mixing_blocks(neighbours.reshape(micro_count, ROWS, neighbours.shape[1]))
    weight_pair = [resident_weight(weights, phase) for phase in range(2)]
    gain_pair = gains[:, 0]
    layer_count = 2 * segments

    state = fields
    saved = [None, None]
    for layer in range(layer_count):
        phase, member = divmod(layer, segments)
        if layer == 0:
            def skip(*_):
                return (
                    jnp.zeros_like(state), jnp.zeros_like(state),
                    jnp.zeros(state.shape, jnp.float32), jnp.zeros((tokens, 1), jnp.float32),
                )

            result, active, squashed, inverse = lax.cond(
                place == 0, layer_forward, skip,
                state, weight_pair[phase], gain_pair[phase], mixing,
            )
        else:
            result, active, squashed, inverse = layer_forward(
                state, weight_pair[phase], gain_pair[phase], mixing
            )
        values = (state, active, squashed, inverse)
        if member == 0:
            saved[phase] = values
        else:
            mine = place == member
            saved[phase] = tuple(jnp.where(mine, new, old) for new, old in zip(values, saved[phase]))
        if layer + 1 < layer_count:
            state = hop(result, layer % segments, (layer + 1) % segments)
        else:
            state = result
        if layer == segments - 1:
            squashed_all = lax.all_gather(saved[0][2], "dp", tiled=True)
            state, squashed_all = lax.optimization_barrier((state, squashed_all))

    upper = ((state.astype(jnp.float32) - targets.astype(jnp.float32)) * scale_top).astype(jnp.bfloat16)

    dpre_saved = [None, None]
    for layer in reversed(range(1, layer_count)):
        phase, member = divmod(layer, segments)
        residual, _, squashed, inverse = saved[phase]
        lower, dbefore = layer_backward(
            residual, squashed, inverse, weight_pair[phase], gain_pair[phase], mixing, upper
        )
        if member == segments - 1:
            dpre_saved[phase] = dbefore
        else:
            dpre_saved[phase] = jnp.where(place == member, dbefore, dpre_saved[phase])
        if layer > 1:
            upper = hop(lower, layer % segments, (layer - 1) % segments)
        if layer == segments:
            early = jnp.concatenate([saved[1][1], dpre_saved[1], saved[0][1]], axis=1)
            early_all = lax.all_gather(early, "dp", tiled=True)
            upper, early_all = lax.optimization_barrier((upper, early_all))

    rows = width // data_groups
    arrived = jnp.stack([
        lax.ppermute(
            lower, ("segment", "dp"),
            [(data_groups + source, (source + shift) % data_groups) for source in range(data_groups)],
        )
        for shift in range(data_groups)
    ])
    reversed_blocks = arrived[::-1]
    doubled = jnp.concatenate([reversed_blocks, reversed_blocks], axis=0)
    upper_all = lax.dynamic_slice_in_dim(doubled, data_groups - 1 - group, data_groups, axis=0)
    upper_all = upper_all.reshape(data_groups * tokens, width).astype(jnp.float32)
    dpre_first = (upper_all * (1.0 - squashed_all * squashed_all)).astype(jnp.bfloat16)
    late_all = jnp.where(place == 0, dpre_first, lax.all_gather(dpre_saved[0], "dp", tiled=True))
    act_rows = jnp.stack([
        lax.dynamic_slice_in_dim(early_all, 2 * width + group * rows, rows, axis=1),
        lax.dynamic_slice_in_dim(early_all, group * rows, rows, axis=1),
    ])
    dpre_all = jnp.stack([late_all, early_all[:, width:2 * width]])
    grads = lax.dot_general(
        act_rows, dpre_all, (((1,), (1,)), ((0,), (0,))), preferred_element_type=jnp.float32
    ).astype(jnp.bfloat16)
    return grads[:, None]


def solution(mesh):
    return jax.shard_map(
        on_device,
        mesh=mesh,
        in_specs=(
            P(("groups", "dp"), None),
            P(("groups", "dp"), None),
            P(("groups", "dp"), None),
            P(None, "segment", None, None),
            P(None, "segment", None),
        ),
        out_specs=P("groups", "segment", "dp", None),
        check_vma=False,
    )
```

```python
import math

import jax
import jax.numpy as jnp
from jax import lax
from jax.experimental import pallas as pl
from jax.experimental.pallas import tpu as pltpu
from jax.sharding import PartitionSpec as P

ROWS = 8


EPSILON = 1e-06


def mixing_blocks(neighbour_rows):
    positions = jnp.arange(neighbour_rows.shape[1], dtype=jnp.int32)
    matches = (neighbour_rows[:, :, :, None] == positions[None, None, None, :]).astype(jnp.float32)
    return jnp.sum(matches, axis=2) * (0.5 / neighbour_rows.shape[2])


def mix_apply(mixing, values):
    micro = mixing.shape[0]
    blocks = values.reshape(micro, ROWS, values.shape[-1])
    mixed = jnp.einsum("bik,bkd->bid", mixing, blocks, precision=lax.Precision.HIGHEST)
    return mixed.reshape(values.shape)


def mix_apply_t(mixing, values):
    micro = mixing.shape[0]
    blocks = values.reshape(micro, ROWS, values.shape[-1])
    mixed = jnp.einsum("bki,bkd->bid", mixing, blocks, precision=lax.Precision.HIGHEST)
    return mixed.reshape(values.shape)


def layer_forward(residual, weight, gain_row, mixing):
    widened = residual.astype(jnp.float32)
    inverse = lax.rsqrt(jnp.mean(widened * widened, axis=-1, keepdims=True) + EPSILON)
    normed = widened * inverse * gain_row
    blended = 0.5 * normed + mix_apply(mixing, normed)
    active = blended.astype(jnp.bfloat16)
    before = jnp.dot(active, weight, preferred_element_type=jnp.float32)
    squashed = jnp.tanh(before)
    return ((widened + squashed).astype(jnp.bfloat16), active, squashed, inverse)


def layer_backward(residual, squashed, inverse, weight, gain_row, mixing, upper_grad):
    widened = residual.astype(jnp.float32)
    above = upper_grad.astype(jnp.float32)
    dbefore = (above * (1.0 - squashed * squashed)).astype(jnp.bfloat16)
    dblend = lax.dot_general(
        dbefore, weight, (((1,), (1,)), ((), ())), preferred_element_type=jnp.float32
    )
    dnormed = (0.5 * dblend + mix_apply_t(mixing, dblend)) * gain_row
    inner_mean = jnp.mean(dnormed * widened, axis=-1, keepdims=True)
    lower_grad = above + inverse * dnormed - widened * (inverse * inverse * inverse) * inner_mean
    return (lower_grad.astype(jnp.bfloat16), dbefore)


def fetch_kernel(phase, weights_hbm, out_vmem, sem):
    copy = pltpu.make_async_copy(weights_hbm.at[phase, 0], out_vmem, sem)
    copy.start()
    copy.wait()


def resident_weight(weights, phase):
    width = weights.shape[-1]
    return pl.pallas_call(
        lambda *refs: fetch_kernel(phase, *refs),
        in_specs=[pl.BlockSpec(memory_space=pl.ANY)],
        out_specs=pl.BlockSpec(memory_space=pltpu.VMEM),
        out_shape=jax.ShapeDtypeStruct((width, width), weights.dtype),
        scratch_shapes=[pltpu.SemaphoreType.DMA(())],
    )(weights)


def hop(array, source, target):
    count = lax.axis_size("segment")
    shift = (target - source) % count
    return lax.ppermute(array, "segment", [(i, (i + shift) % count) for i in range(count)])


def on_device(fields, targets, neighbours, weights, gains):
    segments = lax.axis_size("segment")
    data_groups = lax.axis_size("dp")
    place = lax.axis_index("segment")
    group = lax.axis_index("dp")
    tokens, width = fields.shape
    micro_count = tokens // ROWS
    scale_top = 1.0 / math.sqrt(tokens * data_groups)
    mixing = mixing_blocks(neighbours.reshape(micro_count, ROWS, neighbours.shape[1]))
    weight_pair = [resident_weight(weights, phase) for phase in range(2)]
    gain_pair = gains[:, 0]
    layer_count = 2 * segments

    state = fields
    saved = [None, None]
    for layer in range(layer_count):
        phase, member = divmod(layer, segments)
        if layer == 0:
            def skip(*_):
                return (
                    jnp.zeros_like(state), jnp.zeros_like(state),
                    jnp.zeros(state.shape, jnp.float32), jnp.zeros((tokens, 1), jnp.float32),
                )

            result, active, squashed, inverse = lax.cond(
                place == 0, layer_forward, skip,
                state, weight_pair[phase], gain_pair[phase], mixing,
            )
        else:
            result, active, squashed, inverse = layer_forward(
                state, weight_pair[phase], gain_pair[phase], mixing
            )
        values = (state, active, squashed, inverse)
        if member == 0:
            saved[phase] = values
        else:
            mine = place == member
            saved[phase] = tuple(jnp.where(mine, new, old) for new, old in zip(values, saved[phase]))
        if layer + 1 < layer_count:
            state = hop(result, layer % segments, (layer + 1) % segments)
        else:
            state = result

    upper = ((state.astype(jnp.float32) - targets.astype(jnp.float32)) * scale_top).astype(jnp.bfloat16)

    dpre_saved = [None, None]
    for layer in reversed(range(layer_count)):
        phase, member = divmod(layer, segments)
        residual, _, squashed, inverse = saved[phase]
        lower, dbefore = layer_backward(
            residual, squashed, inverse, weight_pair[phase], gain_pair[phase], mixing, upper
        )
        if member == segments - 1:
            dpre_saved[phase] = dbefore
        else:
            dpre_saved[phase] = jnp.where(place == member, dbefore, dpre_saved[phase])
        if layer > 0:
            upper = hop(lower, layer % segments, (layer - 1) % segments)
        if layer == segments:
            early = jnp.concatenate([saved[1][1], dpre_saved[1], saved[0][1]], axis=1)
            early_all = lax.all_gather(early, "dp", tiled=True)
            upper, early_all = lax.optimization_barrier((upper, early_all))

    rows = width // data_groups
    late_all = lax.all_gather(dpre_saved[0], "dp", tiled=True)
    act_rows = jnp.stack([
        lax.dynamic_slice_in_dim(early_all, 2 * width + group * rows, rows, axis=1),
        lax.dynamic_slice_in_dim(early_all, group * rows, rows, axis=1),
    ])
    dpre_all = jnp.stack([late_all, early_all[:, width:2 * width]])
    grads = lax.dot_general(
        act_rows, dpre_all, (((1,), (1,)), ((0,), (0,))), preferred_element_type=jnp.float32
    ).astype(jnp.bfloat16)
    return grads[:, None]


def solution(mesh):
    return jax.shard_map(
        on_device,
        mesh=mesh,
        in_specs=(
            P(("groups", "dp"), None),
            P(("groups", "dp"), None),
            P(("groups", "dp"), None),
            P(None, "segment", None, None),
            P(None, "segment", None),
        ),
        out_specs=P("groups", "segment", "dp", None),
        check_vma=False,
    )
```

```python
import math

import jax
import jax.numpy as jnp
from jax import lax
from jax.experimental import pallas as pl
from jax.experimental.pallas import tpu as pltpu
from jax.sharding import PartitionSpec as P

ROWS = 8


EPSILON = 1e-06


def mixing_blocks(neighbour_rows):
    positions = jnp.arange(neighbour_rows.shape[1], dtype=jnp.int32)
    matches = (neighbour_rows[:, :, :, None] == positions[None, None, None, :]).astype(jnp.float32)
    return jnp.sum(matches, axis=2) * (0.5 / neighbour_rows.shape[2])


def mix_apply(mixing, values):
    micro = mixing.shape[0]
    blocks = values.reshape(micro, ROWS, values.shape[-1])
    mixed = jnp.einsum("bik,bkd->bid", mixing, blocks, precision=lax.Precision.HIGHEST)
    return mixed.reshape(values.shape)


def mix_apply_t(mixing, values):
    micro = mixing.shape[0]
    blocks = values.reshape(micro, ROWS, values.shape[-1])
    mixed = jnp.einsum("bki,bkd->bid", mixing, blocks, precision=lax.Precision.HIGHEST)
    return mixed.reshape(values.shape)


def layer_forward(residual, weight, gain_row, mixing):
    widened = residual.astype(jnp.float32)
    inverse = lax.rsqrt(jnp.mean(widened * widened, axis=-1, keepdims=True) + EPSILON)
    normed = widened * inverse * gain_row
    blended = 0.5 * normed + mix_apply(mixing, normed)
    active = blended.astype(jnp.bfloat16)
    before = jnp.dot(active, weight, preferred_element_type=jnp.float32)
    squashed = jnp.tanh(before)
    return ((widened + squashed).astype(jnp.bfloat16), active, squashed, inverse)


def layer_backward(residual, squashed, inverse, weight, gain_row, mixing, upper_grad):
    widened = residual.astype(jnp.float32)
    above = upper_grad.astype(jnp.float32)
    dbefore = (above * (1.0 - squashed * squashed)).astype(jnp.bfloat16)
    dblend = lax.dot_general(
        dbefore, weight, (((1,), (1,)), ((), ())), preferred_element_type=jnp.float32
    )
    dnormed = (0.5 * dblend + mix_apply_t(mixing, dblend)) * gain_row
    inner_mean = jnp.mean(dnormed * widened, axis=-1, keepdims=True)
    lower_grad = above + inverse * dnormed - widened * (inverse * inverse * inverse) * inner_mean
    return (lower_grad.astype(jnp.bfloat16), dbefore)


def fetch_kernel(phase, weights_hbm, out_vmem, sem):
    copy = pltpu.make_async_copy(weights_hbm.at[phase, 0], out_vmem, sem)
    copy.start()
    copy.wait()


def resident_weight(weights, phase):
    width = weights.shape[-1]
    return pl.pallas_call(
        lambda *refs: fetch_kernel(phase, *refs),
        in_specs=[pl.BlockSpec(memory_space=pl.ANY)],
        out_specs=pl.BlockSpec(memory_space=pltpu.VMEM),
        out_shape=jax.ShapeDtypeStruct((width, width), weights.dtype),
        scratch_shapes=[pltpu.SemaphoreType.DMA(())],
    )(weights)


def hop(array, source, target):
    return lax.ppermute(array, "segment", [(source, target)])


def on_device(fields, targets, neighbours, weights, gains):
    segments = lax.axis_size("segment")
    data_groups = lax.axis_size("dp")
    place = lax.axis_index("segment")
    group = lax.axis_index("dp")
    tokens, width = fields.shape
    micro_count = tokens // ROWS
    scale_top = 1.0 / math.sqrt(tokens * data_groups)
    mixing = mixing_blocks(neighbours.reshape(micro_count, ROWS, neighbours.shape[1]))
    weight_pair = [resident_weight(weights, phase) for phase in range(2)]
    gain_pair = gains[:, 0]
    layer_count = 2 * segments

    state = fields
    saved = [None, None]
    for layer in range(layer_count):
        phase, member = divmod(layer, segments)
        if layer == 0:
            widened = state.astype(jnp.float32)
            inverse = lax.rsqrt(jnp.mean(widened * widened, axis=-1, keepdims=True) + EPSILON)
            normed = widened * inverse * gain_pair[phase]
            active = (0.5 * normed + mix_apply(mixing, normed)).astype(jnp.bfloat16)

            def project(active, weight, widened):
                squashed = jnp.tanh(jnp.dot(active, weight, preferred_element_type=jnp.float32))
                return (widened + squashed).astype(jnp.bfloat16), squashed

            def skip(active, weight, widened):
                return jnp.zeros_like(active), jnp.zeros(active.shape, jnp.float32)

            result, squashed = lax.cond(place == 0, project, skip, active, weight_pair[phase], widened)
        else:
            result, active, squashed, inverse = layer_forward(
                state, weight_pair[phase], gain_pair[phase], mixing
            )
        values = (state, active, squashed, inverse)
        if member == 0:
            saved[phase] = values
        else:
            mine = place == member
            saved[phase] = tuple(jnp.where(mine, new, old) for new, old in zip(values, saved[phase]))
        if layer + 1 < layer_count:
            state = hop(result, layer % segments, (layer + 1) % segments)
        else:
            state = result

    upper = ((state.astype(jnp.float32) - targets.astype(jnp.float32)) * scale_top).astype(jnp.bfloat16)

    dpre_saved = [None, None]
    for layer in reversed(range(layer_count)):
        phase, member = divmod(layer, segments)
        residual, _, squashed, inverse = saved[phase]
        lower, dbefore = layer_backward(
            residual, squashed, inverse, weight_pair[phase], gain_pair[phase], mixing, upper
        )
        if member == segments - 1:
            dpre_saved[phase] = dbefore
        else:
            dpre_saved[phase] = jnp.where(place == member, dbefore, dpre_saved[phase])
        if layer > 0:
            upper = hop(lower, layer % segments, (layer - 1) % segments)
        if layer == segments:
            early = jnp.concatenate([saved[1][1], dpre_saved[1], saved[0][1]], axis=1)
            early_all = lax.all_gather(early, "dp", tiled=True)
            upper, early_all = lax.optimization_barrier((upper, early_all))

    rows = width // data_groups
    late_all = lax.all_gather(dpre_saved[0], "dp", tiled=True)
    act_rows = jnp.stack([
        lax.dynamic_slice_in_dim(early_all, 2 * width + group * rows, rows, axis=1),
        lax.dynamic_slice_in_dim(early_all, group * rows, rows, axis=1),
    ])
    dpre_all = jnp.stack([late_all, early_all[:, width:2 * width]])
    grads = lax.dot_general(
        act_rows, dpre_all, (((1,), (1,)), ((0,), (0,))), preferred_element_type=jnp.float32
    ).astype(jnp.bfloat16)
    return grads[:, None]


def solution(mesh):
    return jax.shard_map(
        on_device,
        mesh=mesh,
        in_specs=(
            P(("groups", "dp"), None),
            P(("groups", "dp"), None),
            P(("groups", "dp"), None),
            P(None, "segment", None, None),
            P(None, "segment", None),
        ),
        out_specs=P("groups", "segment", "dp", None),
        check_vma=False,
    )
```
